32 devices in a mesh: grp: 8 (over y, x, core), sub: 4 (over z).
Axes of the slice: x: 2, y: 2, z: 4, core: 2. Of those that a mesh axis runs over, the one named last changes fastest.
Arguments:
- tokens: bfloat16 [128, 32, 256], P(('grp', 'sub')), may hold values from -64 to 64
- proj_weight: bfloat16 [256, 256], replicated, may hold values from -2 to 2
- match_grad: bfloat16 [4096, 1024], P(('grp', 'sub')), may hold values from -3072 to 3072
- edge_first: int32 [4096], P(('grp', 'sub')), may hold values from 0 to 15, as said below
- pair_second_image: int32 [4096], P(('grp', 'sub')), may hold values from 0 to 31, as said below
- send_pick: int32 [1024], P(('grp', 'sub')), may hold values from 0 to 3, as said below
Outputs:
- token_grad: bfloat16 [128, 32, 256], P(('grp', 'sub'))
The draws below stay inside these ranges and needn't reach their ends.
Inputs may be any that keep to these rules, and one draw needn't show every extreme that they name: On each device the pairs (edge_first, pair_second_image) are distinct. `pair_second_image`: on each device every receive slot 0 to 31 is named by at least one pair. `send_pick`: for each device and each index p of grp, the 4 entries of its send slots p * 4 to p * 4 + 3 name different images.
All inputs are finite; a program needn't handle non-finite values.
Results may differ from the reference program's by a relative error of at most 0.017.
Values may be sent and summed in bfloat16 or wider, within the bound.
No kernel may reach another device: no remote copies, remote signals or barrier semaphores. Data moves between devices by JAX's collectives and lax.ppermute only.
A program may use at most 64 MiB of HBM per device.

```python
import math
import jax
import jax.numpy as jnp
from jax import lax

D = 256
L = 32
IMG_DEV = 4
EDGE_DEV = 128
SLOTS = 4
RECV = 32
GROUP_IMG = 16
IMAGES = 128
EDGES = 4096
SENDS = 1024
N_GRP = 8
N_SUB = 4


def feature_levels(key):
    return jax.random.uniform(jax.random.fold_in(key, 17), (D,), jnp.float32, 0.0, 1.0)


def draw_tokens(key, part):
    random_key_root, key_row = jax.random.split(jax.random.fold_in(key, 7), 2)
    level = feature_levels(key)
    diag_size = 1.0 - 0.4 * level
    base = jnp.clip(jax.random.normal(random_key_root, (IMAGES, L, D), jnp.float32), -4.0, 4.0)
    row_scale = jnp.exp(jax.random.uniform(key_row, (IMAGES, L, 1), jnp.float32, 0.0, math.log(10.0)))
    col_scale = 0.06 * jnp.exp(level * math.log(10.0)) / diag_size
    return jnp.clip(base * row_scale * col_scale[None, None, :], -64.0, 64.0).astype(jnp.bfloat16)


def draw_proj_weight(key, part):
    key_sign, key_off = jax.random.split(jax.random.fold_in(key, 3))
    level = feature_levels(key)
    diag_size = 1.0 - 0.4 * level
    signs = jnp.where(jax.random.randint(key_sign, (D,), 0, 2, dtype=jnp.int32) == 1, 1.0, -1.0).astype(jnp.float32)
    off_diag = jnp.clip(jax.random.normal(key_off, (D, D), jnp.float32), -4.0, 4.0) * (0.3 / math.sqrt(D))
    index = jnp.arange(D, dtype=jnp.int32)
    on_diag = index[:, None] == index[None, :]
    weight = jnp.where(on_diag, (signs * diag_size)[None, :], off_diag)
    return jnp.clip(weight, -2.0, 2.0).astype(jnp.bfloat16)


def edge_table(key):
    base_key = jax.random.fold_in(key, 11)
    pair_count = GROUP_IMG * RECV

    def one_block(block_index):
        block_key = jax.random.fold_in(base_key, block_index)
        key_noise, key_hub, key_anchor = jax.random.split(block_key, 3)
        noise = jax.random.randint(key_noise, (GROUP_IMG, RECV), 0, 1024, dtype=jnp.int32)
        hub = jax.random.randint(key_hub, (1, RECV), 0, 4, dtype=jnp.int32) * 1024
        anchor_row = jax.random.randint(key_anchor, (RECV,), 0, GROUP_IMG, dtype=jnp.int32)
        anchor = (jnp.arange(GROUP_IMG, dtype=jnp.int32)[:, None] == anchor_row[None, :]).astype(jnp.int32) * 8192
        score = (noise + hub + anchor).reshape(pair_count) * pair_count + jnp.arange(pair_count, dtype=jnp.int32)
        _, picked = lax.top_k(score, EDGE_DEV)
        picked = picked.astype(jnp.int32)
        return (picked // RECV, picked % RECV)
    first_images, seconds = lax.map(one_block, jnp.arange(EDGES // EDGE_DEV, dtype=jnp.int32))
    return (first_images.reshape(EDGES).astype(jnp.int32), seconds.reshape(EDGES).astype(jnp.int32))


def draw_edge_first(key, part):
    return edge_table(key)[0]


def draw_pair_second_image(key, part):
    return edge_table(key)[1]


def draw_send_pick(key, part):
    keys = jax.random.split(jax.random.fold_in(key, 5), SENDS // SLOTS)

    def one_peer(peer_key):
        return jax.random.permutation(peer_key, IMG_DEV)[:SLOTS].astype(jnp.int32)
    return jax.vmap(one_peer)(keys).reshape(SENDS).astype(jnp.int32)


def block_levels(rng, dims, cuts, least, top_value):
    def one(axis_at, blocks):
        heights = jax.random.uniform(jax.random.fold_in(jax.random.fold_in(rng, 6), axis_at), (blocks,), jnp.float32, least / len(cuts), top_value / len(cuts))
        return jnp.repeat(jnp.exp(heights), dims[axis_at] // blocks).reshape((-1,) + (1,) * (len(dims) - axis_at - 1))

    factor_of = one(*cuts[0])
    for cut in cuts[1:]:
        factor_of = factor_of * one(*cut)
    return factor_of


def gaussian(key, extent, deviation, bound, pieces=(), kind=jnp.bfloat16):
    array = jax.random.normal(key, extent, jnp.float32) * deviation
    if len(pieces) > 0:
        array = block_levels(key, extent, pieces, -0.22, 0.18) * array
    return jnp.clip(array, min=-bound, max=bound).astype(kind)


def setup_inputs(seed: int = 0) -> dict:
    key_of = jax.random.split(jax.random.key(seed), 7)
    return {
        "tokens": draw_tokens(jax.random.fold_in(key_of[6], 71), 0),
        "proj_weight": draw_proj_weight(jax.random.fold_in(key_of[6], 71), 0),
        "match_grad": gaussian(key_of[2], (EDGES, L * L), 512.0, 3072.0, ((0, 32),)),
        "edge_first": draw_edge_first(jax.random.fold_in(key_of[6], 71), 0),
        "pair_second_image": draw_pair_second_image(jax.random.fold_in(key_of[6], 71), 0),
        "send_pick": draw_send_pick(jax.random.fold_in(key_of[6], 71), 0),
    }


EPSILON = 1e-05
SOFTMAX_COOLING = 0.1

def normalize(tokens_flat, proj_weight):
    feature = jnp.dot(tokens_flat, proj_weight, preferred_element_type=jnp.float32)
    inv_rms = lax.rsqrt(lax.optimization_barrier(jnp.mean(feature * feature, axis=-1, keepdims=True)) + EPSILON)
    return (feature * inv_rms, inv_rms)

def edge_terms(first_image_features, second_feats, match_block):
    score_scale = 1.0 / (first_image_features.shape[-1] * SOFTMAX_COOLING)
    first_wide = first_image_features.astype(jnp.float32)
    second_wide = second_feats.astype(jnp.float32)
    scores = jnp.einsum('eid,ejd->eij', first_wide, second_wide) * score_scale
    expo = jnp.exp(scores)
    rows = expo / lax.optimization_barrier(jnp.sum(expo, axis=2, keepdims=True))
    cols = expo / lax.optimization_barrier(jnp.sum(expo, axis=1, keepdims=True))
    incoming_gradient = match_block.astype(jnp.float32)
    d_rows = incoming_gradient * cols
    d_cols = incoming_gradient * rows
    d_scores = rows * (d_rows - lax.optimization_barrier(jnp.sum(d_rows * rows, axis=2, keepdims=True))) + cols * (d_cols - lax.optimization_barrier(jnp.sum(d_cols * cols, axis=1, keepdims=True)))
    d_scaled = lax.optimization_barrier((d_scores * score_scale).astype(jnp.bfloat16)).astype(jnp.float32)
    grad_first = jnp.einsum('eij,ejd->eid', d_scaled, second_wide)
    grad_second = jnp.einsum('eij,eid->ejd', d_scaled, first_wide)
    return (grad_first, grad_second)

def reference(tokens, proj_weight, match_grad, edge_first, pair_second_image, send_pick):
    images = tokens.shape[0]
    normed, inv_rms = normalize(tokens.reshape(images * L, D), proj_weight)
    normed_b = normed.astype(jnp.bfloat16).reshape(images, L, D)
    devices = N_GRP * N_SUB
    picks_all = send_pick.reshape(devices, RECV)
    grads_all = match_grad.reshape(devices, EDGE_DEV, L, L)
    firsts_all = edge_first.reshape(devices, EDGE_DEV)
    seconds_all = pair_second_image.reshape(devices, EDGE_DEV)
    slot_ids = jnp.arange(RECV, dtype=jnp.int32)

    def device_step(total, inputs):
        device, grads, first_images, seconds = inputs
        group = device // N_SUB
        member = device % N_SUB
        pool = lax.dynamic_slice_in_dim(normed_b, (group * GROUP_IMG).astype(jnp.int32), GROUP_IMG, 0)
        senders = slot_ids // SLOTS * N_SUB + member
        picked = picks_all[senders, group * SLOTS + slot_ids % SLOTS]
        slot_images = (senders * IMG_DEV + picked).astype(jnp.int32)
        received = normed_b[slot_images]
        grad_first, grad_second = edge_terms(pool[first_images], received[seconds], grads)
        pool_part = jax.ops.segment_sum(grad_first, first_images, num_segments=GROUP_IMG)
        slot_part = jax.ops.segment_sum(grad_second, seconds, num_segments=RECV)
        pool_round = lax.optimization_barrier(pool_part.astype(jnp.bfloat16)).astype(jnp.float32)
        slot_round = lax.optimization_barrier(slot_part.astype(jnp.bfloat16)).astype(jnp.float32)
        start = (group * GROUP_IMG).astype(jnp.int32)
        block = lax.dynamic_slice_in_dim(total, start, GROUP_IMG, 0) + pool_round
        total = lax.dynamic_update_slice_in_dim(total, block, start, 0)
        total = total.at[slot_images].add(slot_round)
        return (total, None)
    total, _ = lax.scan(device_step, jnp.zeros((images, L, D), jnp.float32), (jnp.arange(devices, dtype=jnp.int32), grads_all, firsts_all, seconds_all))
    incoming_gradient = total.reshape(images * L, D)
    feature_grad = inv_rms * (incoming_gradient - normed * lax.optimization_barrier(jnp.mean(incoming_gradient * normed, axis=-1, keepdims=True)))
    token_grad = jnp.dot(feature_grad.astype(jnp.bfloat16), proj_weight.T, preferred_element_type=jnp.float32)
    return token_grad.astype(jnp.bfloat16).reshape(images, L, D)
```

```python
import jax
import jax.numpy as jnp
from jax import lax
from jax.sharding import PartitionSpec as P

EPSILON = 1e-05
SOFTMAX_COOLING = 0.1
SUB_MODE = "perm"
GRP_MODE = "perm"
CHUNK_ELEMS = 1 << 19


def normalize(tokens, proj_weight):
    image_count, length, feat_width = tokens.shape
    feature = jnp.dot(
        tokens.reshape(image_count * length, feat_width),
        proj_weight,
        preferred_element_type=jnp.float32,
    )
    inv_rms = lax.rsqrt(jnp.mean(feature * feature, axis=-1, keepdims=True) + EPSILON)
    normed = feature * inv_rms
    return (normed, inv_rms, normed.astype(jnp.bfloat16).reshape(image_count, length, feat_width))


def shift(count, step):
    return [(i, (i + step) % count) for i in range(count)]


def dense_terms(pool_c, received, grads_c):
    score_scale = 1.0 / (pool_c.shape[-1] * SOFTMAX_COOLING)
    scores = (
        jnp.einsum("ird,jcd->ijrc", pool_c, received, preferred_element_type=jnp.float32)
        * score_scale
    )
    expo = jnp.exp(scores)
    rows = expo / jnp.sum(expo, axis=3, keepdims=True)
    cols = expo / jnp.sum(expo, axis=2, keepdims=True)
    d_rows = grads_c * cols
    d_cols = grads_c * rows
    d_scores = rows * (d_rows - jnp.sum(d_rows * rows, axis=3, keepdims=True)) + cols * (
        d_cols - jnp.sum(d_cols * cols, axis=2, keepdims=True)
    )
    d_scaled = (d_scores * score_scale).astype(jnp.bfloat16)
    pool_part = jnp.einsum("ijrc,jcd->ird", d_scaled, received, preferred_element_type=jnp.float32)
    slot_part = jnp.einsum("ijrc,ird->jcd", d_scaled, pool_c, preferred_element_type=jnp.float32)
    return pool_part, slot_part


def local(n_grp, n_sub, tokens, proj_weight, match_grad, edge_first, pair_second_image, send_pick):
    img_count, length, feat_width = tokens.shape
    recv = send_pick.shape[0]
    slots = recv // n_grp
    group_img = img_count * n_sub
    edge_count = edge_first.shape[0]
    grp_at = lax.axis_index("grp")
    sub_at = lax.axis_index("sub")

    normed, inv_rms, normed_b = normalize(tokens, proj_weight)

    if SUB_MODE == "perm":
        pool = jnp.concatenate(
            [normed_b] + [lax.ppermute(normed_b, "sub", shift(n_sub, k)) for k in range(1, n_sub)],
            axis=0,
        )
        first_at = ((sub_at - edge_first // img_count) % n_sub) * img_count + edge_first % img_count
    else:
        pool = lax.all_gather(normed_b, "sub", axis=0, tiled=True)
        first_at = edge_first

    picks = send_pick.reshape(n_grp, slots)
    flat_b = normed_b.reshape(img_count, length * feat_width)
    if GRP_MODE == "perm":
        order = picks[(grp_at + jnp.arange(n_grp, dtype=jnp.int32)) % n_grp].reshape(recv)
    else:
        order = send_pick
    pick_onehot = (order[:, None] == jnp.arange(img_count, dtype=jnp.int32)[None, :]).astype(
        jnp.bfloat16
    )
    outgoing = jnp.dot(pick_onehot, flat_b, preferred_element_type=jnp.float32).astype(jnp.bfloat16)
    outgoing = outgoing.reshape(recv, length, feat_width)
    if GRP_MODE == "perm":
        received = jnp.concatenate(
            [outgoing[:slots]]
            + [
                lax.ppermute(outgoing[k * slots : (k + 1) * slots], "grp", shift(n_grp, k))
                for k in range(1, n_grp)
            ],
            axis=0,
        )
        second_at = ((grp_at - pair_second_image // slots) % n_grp) * slots + pair_second_image % slots
    else:
        received = lax.all_to_all(outgoing, "grp", split_axis=0, concat_axis=0, tiled=True)
        second_at = pair_second_image

    pair_at = first_at * recv + second_at
    chunk = group_img
    while chunk > 1 and (chunk * recv * length * length > CHUNK_ELEMS or group_img % chunk):
        chunk -= 1
    n_chunks = group_img // chunk

    def one_chunk(chunk_index):
        base = chunk_index * (chunk * recv)
        scatter = (
            lax.broadcasted_iota(jnp.int32, (chunk * recv, edge_count), 0) + base == pair_at[None, :]
        ).astype(jnp.bfloat16)
        grads_c = jnp.dot(scatter, match_grad, preferred_element_type=jnp.float32).reshape(
            chunk, recv, length, length
        )
        pool_c = lax.dynamic_slice_in_dim(pool, chunk_index * chunk, chunk, 0)
        return dense_terms(pool_c, received, grads_c)

    if n_chunks == 1:
        pool_total, slot_total = one_chunk(0)
    else:

        def body(carry, chunk_index):
            pool_part, slot_part = one_chunk(chunk_index)
            return carry + slot_part, pool_part.astype(jnp.bfloat16)

        slot_total, pool_parts = lax.scan(
            body,
            jnp.zeros((recv, length, feat_width), jnp.float32),
            jnp.arange(n_chunks, dtype=jnp.int32),
        )
        pool_total = pool_parts.reshape(group_img, length, feat_width)
    pool_b = pool_total.astype(jnp.bfloat16)
    slot_b = slot_total.astype(jnp.bfloat16)

    if SUB_MODE == "perm":
        owned = pool_b[:img_count].astype(jnp.float32)
        for k in range(1, n_sub):
            owned = owned + lax.ppermute(
                pool_b[k * img_count : (k + 1) * img_count], "sub", shift(n_sub, -k)
            ).astype(jnp.float32)
    else:
        owned = lax.psum_scatter(pool_b, "sub", scatter_dimension=0, tiled=True).astype(jnp.float32)

    if GRP_MODE == "perm":
        returned = jnp.concatenate(
            [slot_b[:slots]]
            + [
                lax.ppermute(slot_b[k * slots : (k + 1) * slots], "grp", shift(n_grp, -k))
                for k in range(1, n_grp)
            ],
            axis=0,
        )
    else:
        returned = lax.all_to_all(slot_b, "grp", split_axis=0, concat_axis=0, tiled=True)
    incoming_gradient = owned.reshape(img_count, length * feat_width) + jnp.dot(
        pick_onehot.T, returned.reshape(recv, length * feat_width), preferred_element_type=jnp.float32
    )
    incoming_gradient = incoming_gradient.reshape(img_count * length, feat_width)
    feature_grad = (
        inv_rms
        * (
            incoming_gradient
            - normed * jnp.mean(incoming_gradient * normed, axis=-1, keepdims=True)
        )
    ).astype(jnp.bfloat16)
    token_grad = jnp.einsum(
        "nk,dk->nd", feature_grad, proj_weight, preferred_element_type=jnp.float32
    )
    return token_grad.astype(jnp.bfloat16).reshape(img_count, length, feat_width)


def solution(mesh):
    placed = (
        P(("grp", "sub"), None, None),
        P(),
        P(("grp", "sub"), None),
        P(("grp", "sub")),
        P(("grp", "sub")),
        P(("grp", "sub")),
    )
    n_grp = mesh.shape["grp"]
    n_sub = mesh.shape["sub"]

    def run(*args):
        return local(n_grp, n_sub, *args)

    return jax.shard_map(
        run, mesh=mesh, in_specs=placed, out_specs=P(("grp", "sub"), None, None), check_vma=False
    )
```

```python
import functools

import jax
import jax.numpy as jnp
from jax import lax
from jax.experimental import pallas as pl
from jax.experimental.pallas import tpu as pltpu
from jax.sharding import PartitionSpec as P

EPSILON = 1e-05
SOFTMAX_COOLING = 0.1
SUB_MODE = "perm"
GRP_MODE = "perm"


def normalize(tokens, proj_weight):
    image_count, length, feat_width = tokens.shape
    feature = jnp.dot(
        tokens.reshape(image_count * length, feat_width),
        proj_weight,
        preferred_element_type=jnp.float32,
    )
    inv_rms = lax.rsqrt(jnp.mean(feature * feature, axis=-1, keepdims=True) + EPSILON)
    normed = feature * inv_rms
    return (normed, inv_rms, normed.astype(jnp.bfloat16).reshape(image_count, length, feat_width))


def shift(count, step):
    return [(i, (i + step) % count) for i in range(count)]


def lane_group_sum(x, group):
    rows, width = x.shape
    xt = x.T.reshape(width // group, group, rows)
    total = jnp.sum(xt, axis=1, keepdims=True)
    return jnp.broadcast_to(total, (width // group, group, rows)).reshape(width, rows).T


def row_group_sum(x, group):
    rows, width = x.shape
    xr = x.reshape(rows // group, group, width)
    total = jnp.sum(xr, axis=1, keepdims=True)
    return jnp.broadcast_to(total, (rows // group, group, width)).reshape(rows, width)


def softmax_bwd_kernel(group, score_scale, s_ref, g_ref, d_ref):
    expo = jnp.exp(s_ref[...])
    rows = expo / lane_group_sum(expo, group)
    cols = expo / row_group_sum(expo, group)
    grads = g_ref[...].astype(jnp.float32)
    d_rows = grads * cols
    d_cols = grads * rows
    d_scores = rows * (d_rows - lane_group_sum(d_rows * rows, group)) + cols * (
        d_cols - row_group_sum(d_cols * cols, group)
    )
    d_ref[...] = (d_scores * score_scale).astype(jnp.bfloat16)


def softmax_bwd(scores, grads, group, score_scale):
    total_rows, width = scores.shape
    block = 128 if total_rows % 128 == 0 else total_rows
    return pl.pallas_call(
        functools.partial(softmax_bwd_kernel, group, score_scale),
        out_shape=jax.ShapeDtypeStruct((total_rows, width), jnp.bfloat16),
        grid=(total_rows // block,),
        in_specs=[
            pl.BlockSpec((block, width), lambda b: (b, 0)),
            pl.BlockSpec((block, width), lambda b: (b, 0)),
        ],
        out_specs=pl.BlockSpec((block, width), lambda b: (b, 0)),
        compiler_params=pltpu.CompilerParams(vmem_limit_bytes=48 * 1024 * 1024),
        cost_estimate=pl.CostEstimate(
            flops=30 * total_rows * width,
            transcendentals=total_rows * width,
            bytes_accessed=8 * total_rows * width,
        ),
    )(scores, grads)


def local(n_grp, n_sub, tokens, proj_weight, match_grad, edge_first, pair_second_image, send_pick):
    img_count, length, feat_width = tokens.shape
    recv = send_pick.shape[0]
    slots = recv // n_grp
    group_img = img_count * n_sub
    edge_count = edge_first.shape[0]
    grp_at = lax.axis_index("grp")
    sub_at = lax.axis_index("sub")

    normed, inv_rms, normed_b = normalize(tokens, proj_weight)

    if SUB_MODE == "perm":
        pool = jnp.concatenate(
            [normed_b] + [lax.ppermute(normed_b, "sub", shift(n_sub, k)) for k in range(1, n_sub)],
            axis=0,
        )
        first_at = ((sub_at - edge_first // img_count) % n_sub) * img_count + edge_first % img_count
    else:
        pool = lax.all_gather(normed_b, "sub", axis=0, tiled=True)
        first_at = edge_first

    picks = send_pick.reshape(n_grp, slots)
    flat_b = normed_b.reshape(img_count, length * feat_width)
    if GRP_MODE == "perm":
        order = picks[(grp_at + jnp.arange(n_grp, dtype=jnp.int32)) % n_grp].reshape(recv)
    else:
        order = send_pick
    pick_onehot = (order[:, None] == jnp.arange(img_count, dtype=jnp.int32)[None, :]).astype(
        jnp.bfloat16
    )
    outgoing = jnp.dot(pick_onehot, flat_b, preferred_element_type=jnp.float32).astype(jnp.bfloat16)
    outgoing = outgoing.reshape(recv, length, feat_width)
    if GRP_MODE == "perm":
        received = jnp.concatenate(
            [outgoing[:slots]]
            + [
                lax.ppermute(outgoing[k * slots : (k + 1) * slots], "grp", shift(n_grp, k))
                for k in range(1, n_grp)
            ],
            axis=0,
        )
        second_at = ((grp_at - pair_second_image // slots) % n_grp) * slots + pair_second_image % slots
    else:
        received = lax.all_to_all(outgoing, "grp", split_axis=0, concat_axis=0, tiled=True)
        second_at = pair_second_image

    pair_at = first_at * recv + second_at
    scatter = (
        lax.broadcasted_iota(jnp.int32, (group_img * recv, edge_count), 0) == pair_at[None, :]
    ).astype(jnp.bfloat16)
    grads = jnp.dot(scatter, match_grad, preferred_element_type=jnp.float32).astype(jnp.bfloat16)
    grads = grads.reshape(group_img, recv, length, length).transpose(0, 2, 1, 3)
    grads = grads.reshape(group_img * length, recv * length)
    pool2 = pool.reshape(group_img * length, feat_width)
    recv2 = received.reshape(recv * length, feat_width)
    score_scale = 1.0 / (feat_width * SOFTMAX_COOLING)
    scores = (
        lax.dot_general(pool2, recv2, (((1,), (1,)), ((), ())), preferred_element_type=jnp.float32)
        * score_scale
    )
    d_scaled = softmax_bwd(scores, grads, length, score_scale)
    pool_total = jnp.dot(d_scaled, recv2, preferred_element_type=jnp.float32).reshape(
        group_img, length, feat_width
    )
    slot_total = lax.dot_general(
        d_scaled, pool2, (((0,), (0,)), ((), ())), preferred_element_type=jnp.float32
    ).reshape(recv, length, feat_width)
    pool_b = pool_total.astype(jnp.bfloat16)
    slot_b = slot_total.astype(jnp.bfloat16)

    if SUB_MODE == "perm":
        owned = pool_b[:img_count].astype(jnp.float32)
        for k in range(1, n_sub):
            owned = owned + lax.ppermute(
                pool_b[k * img_count : (k + 1) * img_count], "sub", shift(n_sub, -k)
            ).astype(jnp.float32)
    else:
        owned = lax.psum_scatter(pool_b, "sub", scatter_dimension=0, tiled=True).astype(jnp.float32)

    if GRP_MODE == "perm":
        returned = jnp.concatenate(
            [slot_b[:slots]]
            + [
                lax.ppermute(slot_b[k * slots : (k + 1) * slots], "grp", shift(n_grp, -k))
                for k in range(1, n_grp)
            ],
            axis=0,
        )
    else:
        returned = lax.all_to_all(slot_b, "grp", split_axis=0, concat_axis=0, tiled=True)
    incoming_gradient = owned.reshape(img_count, length * feat_width) + jnp.dot(
        pick_onehot.T, returned.reshape(recv, length * feat_width), preferred_element_type=jnp.float32
    )
    incoming_gradient = incoming_gradient.reshape(img_count * length, feat_width)
    feature_grad = (
        inv_rms
        * (
            incoming_gradient
            - normed * jnp.mean(incoming_gradient * normed, axis=-1, keepdims=True)
        )
    ).astype(jnp.bfloat16)
    token_grad = jnp.einsum(
        "nk,dk->nd", feature_grad, proj_weight, preferred_element_type=jnp.float32
    )
    return token_grad.astype(jnp.bfloat16).reshape(img_count, length, feat_width)


def solution(mesh):
    placed = (
        P(("grp", "sub"), None, None),
        P(),
        P(("grp", "sub"), None),
        P(("grp", "sub")),
        P(("grp", "sub")),
        P(("grp", "sub")),
    )
    n_grp = mesh.shape["grp"]
    n_sub = mesh.shape["sub"]

    def run(*args):
        return local(n_grp, n_sub, *args)

    return jax.shard_map(
        run, mesh=mesh, in_specs=placed, out_specs=P(("grp", "sub"), None, None), check_vma=False
    )
```

```python
import functools

import jax
import jax.numpy as jnp
from jax import lax
from jax.experimental import pallas as pl
from jax.experimental.pallas import tpu as pltpu
from jax.sharding import PartitionSpec as P

EPSILON = 1e-05
SOFTMAX_COOLING = 0.1
SUB_MODE = "perm"
GRP_MODE = "perm"


def normalize(tokens, proj_weight):
    image_count, length, feat_width = tokens.shape
    feature = jnp.dot(
        tokens.reshape(image_count * length, feat_width),
        proj_weight,
        preferred_element_type=jnp.float32,
    )
    inv_rms = lax.rsqrt(jnp.mean(feature * feature, axis=-1, keepdims=True) + EPSILON)
    normed = feature * inv_rms
    return (normed, inv_rms, normed.astype(jnp.bfloat16).reshape(image_count, length, feat_width))


def shift(count, step):
    return [(i, (i + step) % count) for i in range(count)]


def lane_group_sum(x, group):
    rows, width = x.shape
    xt = x.T.reshape(width // group, group, rows)
    total = jnp.sum(xt, axis=1, keepdims=True)
    return jnp.broadcast_to(total, (width // group, group, rows)).reshape(width, rows).T


def row_group_sum(x, group):
    rows, width = x.shape
    xr = x.reshape(rows // group, group, width)
    total = jnp.sum(xr, axis=1, keepdims=True)
    return jnp.broadcast_to(total, (rows // group, group, width)).reshape(rows, width)


def softmax_bwd_kernel(group, score_scale, recv, edge_at_ref, s_ref, m_ref, d_ref, g_scr):
    block = pl.program_id(0)
    firsts = s_ref.shape[0] // group

    def place(first, carry):
        row = pl.multiple_of(first * group, group)
        base = (block * firsts + first) * recv
        for second in range(recv):
            g_scr[pl.ds(row, group), second * group : (second + 1) * group] = m_ref[
                edge_at_ref[base + second]
            ].astype(jnp.float32)
        return carry

    lax.fori_loop(0, firsts, place, 0)
    expo = jnp.exp(s_ref[...])
    rows = expo / lane_group_sum(expo, group)
    cols = expo / row_group_sum(expo, group)
    grads = g_scr[...]
    d_rows = grads * cols
    d_cols = grads * rows
    d_scores = rows * (d_rows - lane_group_sum(d_rows * rows, group)) + cols * (
        d_cols - row_group_sum(d_cols * cols, group)
    )
    d_ref[...] = (d_scores * score_scale).astype(jnp.bfloat16)


def softmax_bwd(scores, edge_at, blocks, group, score_scale):
    total_rows, width = scores.shape
    recv = width // group
    block = 128 if total_rows % 128 == 0 else total_rows
    return pl.pallas_call(
        functools.partial(softmax_bwd_kernel, group, score_scale, recv),
        out_shape=jax.ShapeDtypeStruct((total_rows, width), jnp.bfloat16),
        grid_spec=pltpu.PrefetchScalarGridSpec(
            num_scalar_prefetch=1,
            grid=(total_rows // block,),
            in_specs=[
                pl.BlockSpec((block, width), lambda b, e: (b, 0)),
                pl.BlockSpec(blocks.shape, lambda b, e: (0, 0, 0)),
            ],
            out_specs=pl.BlockSpec((block, width), lambda b, e: (b, 0)),
            scratch_shapes=[pltpu.VMEM((block, width), jnp.float32)],
        ),
        compiler_params=pltpu.CompilerParams(vmem_limit_bytes=48 * 1024 * 1024),
        cost_estimate=pl.CostEstimate(
            flops=30 * total_rows * width,
            transcendentals=total_rows * width,
            bytes_accessed=6 * total_rows * width,
        ),
    )(edge_at, scores, blocks)


def local(n_grp, n_sub, tokens, proj_weight, match_grad, edge_first, pair_second_image, send_pick):
    img_count, length, feat_width = tokens.shape
    recv = send_pick.shape[0]
    slots = recv // n_grp
    group_img = img_count * n_sub
    edge_count = edge_first.shape[0]
    grp_at = lax.axis_index("grp")
    sub_at = lax.axis_index("sub")

    normed, inv_rms, normed_b = normalize(tokens, proj_weight)

    if SUB_MODE == "perm":
        pool = jnp.concatenate(
            [normed_b] + [lax.ppermute(normed_b, "sub", shift(n_sub, k)) for k in range(1, n_sub)],
            axis=0,
        )
        first_at = ((sub_at - edge_first // img_count) % n_sub) * img_count + edge_first % img_count
    else:
        pool = lax.all_gather(normed_b, "sub", axis=0, tiled=True)
        first_at = edge_first

    picks = send_pick.reshape(n_grp, slots)
    flat_b = normed_b.reshape(img_count, length * feat_width)
    if GRP_MODE == "perm":
        order = picks[(grp_at + jnp.arange(n_grp, dtype=jnp.int32)) % n_grp].reshape(recv)
    else:
        order = send_pick
    pick_onehot = (order[:, None] == jnp.arange(img_count, dtype=jnp.int32)[None, :]).astype(
        jnp.bfloat16
    )
    outgoing = jnp.dot(pick_onehot, flat_b, preferred_element_type=jnp.float32).astype(jnp.bfloat16)
    outgoing = outgoing.reshape(recv, length, feat_width)
    if GRP_MODE == "perm":
        received = jnp.concatenate(
            [outgoing[:slots]]
            + [
                lax.ppermute(outgoing[k * slots : (k + 1) * slots], "grp", shift(n_grp, k))
                for k in range(1, n_grp)
            ],
            axis=0,
        )
        second_at = ((grp_at - pair_second_image // slots) % n_grp) * slots + pair_second_image % slots
    else:
        received = lax.all_to_all(outgoing, "grp", split_axis=0, concat_axis=0, tiled=True)
        second_at = pair_second_image

    pair_at = first_at * recv + second_at
    edge_ids = jnp.arange(edge_count, dtype=jnp.int32)
    edge_at = jnp.min(
        jnp.where(
            lax.broadcasted_iota(jnp.int32, (group_img * recv, edge_count), 0) == pair_at[None, :],
            edge_ids[None, :],
            edge_count,
        ),
        axis=1,
    )
    blocks = jnp.concatenate(
        [match_grad.reshape(edge_count, length, length), jnp.zeros((1, length, length), match_grad.dtype)],
        axis=0,
    )
    pool2 = pool.reshape(group_img * length, feat_width)
    recv2 = received.reshape(recv * length, feat_width)
    score_scale = 1.0 / (feat_width * SOFTMAX_COOLING)
    scores = (
        lax.dot_general(pool2, recv2, (((1,), (1,)), ((), ())), preferred_element_type=jnp.float32)
        * score_scale
    )
    d_scaled = softmax_bwd(scores, edge_at, blocks, length, score_scale)
    pool_total = jnp.dot(d_scaled, recv2, preferred_element_type=jnp.float32).reshape(
        group_img, length, feat_width
    )
    slot_total = lax.dot_general(
        d_scaled, pool2, (((0,), (0,)), ((), ())), preferred_element_type=jnp.float32
    ).reshape(recv, length, feat_width)
    pool_b = pool_total.astype(jnp.bfloat16)
    slot_b = slot_total.astype(jnp.bfloat16)

    if SUB_MODE == "perm":
        owned = pool_b[:img_count].astype(jnp.float32)
        for k in range(1, n_sub):
            owned = owned + lax.ppermute(
                pool_b[k * img_count : (k + 1) * img_count], "sub", shift(n_sub, -k)
            ).astype(jnp.float32)
    else:
        owned = lax.psum_scatter(pool_b, "sub", scatter_dimension=0, tiled=True).astype(jnp.float32)

    if GRP_MODE == "perm":
        returned = jnp.concatenate(
            [slot_b[:slots]]
            + [
                lax.ppermute(slot_b[k * slots : (k + 1) * slots], "grp", shift(n_grp, -k))
                for k in range(1, n_grp)
            ],
            axis=0,
        )
    else:
        returned = lax.all_to_all(slot_b, "grp", split_axis=0, concat_axis=0, tiled=True)
    incoming_gradient = owned.reshape(img_count, length * feat_width) + jnp.dot(
        pick_onehot.T, returned.reshape(recv, length * feat_width), preferred_element_type=jnp.float32
    )
    incoming_gradient = incoming_gradient.reshape(img_count * length, feat_width)
    feature_grad = (
        inv_rms
        * (
            incoming_gradient
            - normed * jnp.mean(incoming_gradient * normed, axis=-1, keepdims=True)
        )
    ).astype(jnp.bfloat16)
    token_grad = jnp.einsum(
        "nk,dk->nd", feature_grad, proj_weight, preferred_element_type=jnp.float32
    )
    return token_grad.astype(jnp.bfloat16).reshape(img_count, length, feat_width)


def solution(mesh):
    placed = (
        P(("grp", "sub"), None, None),
        P(),
        P(("grp", "sub"), None),
        P(("grp", "sub")),
        P(("grp", "sub")),
        P(("grp", "sub")),
    )
    n_grp = mesh.shape["grp"]
    n_sub = mesh.shape["sub"]

    def run(*args):
        return local(n_grp, n_sub, *args)

    return jax.shard_map(
        run, mesh=mesh, in_specs=placed, out_specs=P(("grp", "sub"), None, None), check_vma=False
    )
```

```python
import functools

import jax
import jax.numpy as jnp
from jax import lax
from jax.experimental import pallas as pl
from jax.experimental.pallas import tpu as pltpu
from jax.sharding import PartitionSpec as P

EPSILON = 1e-05
SOFTMAX_COOLING = 0.1
SUB_MODE = "perm"
GRP_MODE = "a2a"


def normalize(tokens, proj_weight):
    image_count, length, feat_width = tokens.shape
    feature = jnp.dot(
        tokens.reshape(image_count * length, feat_width),
        proj_weight,
        preferred_element_type=jnp.float32,
    )
    inv_rms = lax.rsqrt(jnp.mean(feature * feature, axis=-1, keepdims=True) + EPSILON)
    normed = feature * inv_rms
    return (normed, inv_rms, normed.astype(jnp.bfloat16).reshape(image_count, length, feat_width))


def shift(count, step):
    return [(i, (i + step) % count) for i in range(count)]


def lane_group_sum(x, group):
    rows, width = x.shape
    xt = x.T.reshape(width // group, group, rows)
    total = jnp.sum(xt, axis=1, keepdims=True)
    return jnp.broadcast_to(total, (width // group, group, rows)).reshape(width, rows).T


def row_group_sum(x, group):
    rows, width = x.shape
    xr = x.reshape(rows // group, group, width)
    total = jnp.sum(xr, axis=1, keepdims=True)
    return jnp.broadcast_to(total, (rows // group, group, width)).reshape(rows, width)


def softmax_bwd_kernel(group, score_scale, recv, edge_at_ref, s_ref, m_ref, d_ref, g_scr):
    block = pl.program_id(0)
    firsts = s_ref.shape[0] // group

    def place(first, carry):
        row = pl.multiple_of(first * group, group)
        base = (block * firsts + first) * recv
        for second in range(recv):
            g_scr[pl.ds(row, group), second * group : (second + 1) * group] = m_ref[
                edge_at_ref[base + second]
            ].astype(jnp.float32)
        return carry

    lax.fori_loop(0, firsts, place, 0)
    expo = jnp.exp(s_ref[...])
    rows = expo / lane_group_sum(expo, group)
    cols = expo / row_group_sum(expo, group)
    grads = g_scr[...]
    d_rows = grads * cols
    d_cols = grads * rows
    d_scores = rows * (d_rows - lane_group_sum(d_rows * rows, group)) + cols * (
        d_cols - row_group_sum(d_cols * cols, group)
    )
    d_ref[...] = (d_scores * score_scale).astype(jnp.bfloat16)


def softmax_bwd(scores, edge_at, blocks, group, score_scale):
    total_rows, width = scores.shape
    recv = width // group
    block = 128 if total_rows % 128 == 0 else total_rows
    return pl.pallas_call(
        functools.partial(softmax_bwd_kernel, group, score_scale, recv),
        out_shape=jax.ShapeDtypeStruct((total_rows, width), jnp.bfloat16),
        grid_spec=pltpu.PrefetchScalarGridSpec(
            num_scalar_prefetch=1,
            grid=(total_rows // block,),
            in_specs=[
                pl.BlockSpec((block, width), lambda b, e: (b, 0)),
                pl.BlockSpec(blocks.shape, lambda b, e: (0, 0, 0)),
            ],
            out_specs=pl.BlockSpec((block, width), lambda b, e: (b, 0)),
            scratch_shapes=[pltpu.VMEM((block, width), jnp.float32)],
        ),
        compiler_params=pltpu.CompilerParams(vmem_limit_bytes=48 * 1024 * 1024),
        cost_estimate=pl.CostEstimate(
            flops=30 * total_rows * width,
            transcendentals=total_rows * width,
            bytes_accessed=6 * total_rows * width,
        ),
    )(edge_at, scores, blocks)


def local(n_grp, n_sub, tokens, proj_weight, match_grad, edge_first, pair_second_image, send_pick):
    img_count, length, feat_width = tokens.shape
    recv = send_pick.shape[0]
    slots = recv // n_grp
    group_img = img_count * n_sub
    edge_count = edge_first.shape[0]
    grp_at = lax.axis_index("grp")
    sub_at = lax.axis_index("sub")

    normed, inv_rms, normed_b = normalize(tokens, proj_weight)

    if SUB_MODE == "perm":
        pool = jnp.concatenate(
            [normed_b] + [lax.ppermute(normed_b, "sub", shift(n_sub, k)) for k in range(1, n_sub)],
            axis=0,
        )
        first_at = ((sub_at - edge_first // img_count) % n_sub) * img_count + edge_first % img_count
    elif SUB_MODE == "gather":
        pool = lax.all_gather(normed_b, "sub", axis=0, tiled=True)
        first_at = edge_first
    else:
        pool = lax.all_to_all(
            jnp.concatenate([normed_b] * n_sub, axis=0), "sub", split_axis=0, concat_axis=0, tiled=True
        )
        first_at = edge_first

    picks = send_pick.reshape(n_grp, slots)
    flat_b = normed_b.reshape(img_count, length * feat_width)
    if GRP_MODE == "perm":
        order = picks[(grp_at + jnp.arange(n_grp, dtype=jnp.int32)) % n_grp].reshape(recv)
    else:
        order = send_pick
    pick_onehot = (order[:, None] == jnp.arange(img_count, dtype=jnp.int32)[None, :]).astype(
        jnp.bfloat16
    )
    outgoing = jnp.dot(pick_onehot, flat_b, preferred_element_type=jnp.float32).astype(jnp.bfloat16)
    outgoing = outgoing.reshape(recv, length, feat_width)
    if GRP_MODE == "perm":
        received = jnp.concatenate(
            [outgoing[:slots]]
            + [
                lax.ppermute(outgoing[k * slots : (k + 1) * slots], "grp", shift(n_grp, k))
                for k in range(1, n_grp)
            ],
            axis=0,
        )
        second_at = ((grp_at - pair_second_image // slots) % n_grp) * slots + pair_second_image % slots
    else:
        received = lax.all_to_all(outgoing, "grp", split_axis=0, concat_axis=0, tiled=True)
        second_at = pair_second_image

    pair_at = first_at * recv + second_at
    edge_ids = jnp.arange(edge_count, dtype=jnp.int32)
    edge_at = jnp.min(
        jnp.where(
            lax.broadcasted_iota(jnp.int32, (group_img * recv, edge_count), 0) == pair_at[None, :],
            edge_ids[None, :],
            edge_count,
        ),
        axis=1,
    )
    blocks = jnp.concatenate(
        [match_grad.reshape(edge_count, length, length), jnp.zeros((1, length, length), match_grad.dtype)],
        axis=0,
    )
    pool2 = pool.reshape(group_img * length, feat_width)
    recv2 = received.reshape(recv * length, feat_width)
    score_scale = 1.0 / (feat_width * SOFTMAX_COOLING)
    scores = (
        lax.dot_general(pool2, recv2, (((1,), (1,)), ((), ())), preferred_element_type=jnp.float32)
        * score_scale
    )
    d_scaled = softmax_bwd(scores, edge_at, blocks, length, score_scale)
    pool_total = jnp.dot(d_scaled, recv2, preferred_element_type=jnp.float32).reshape(
        group_img, length, feat_width
    )
    slot_total = lax.dot_general(
        d_scaled, pool2, (((0,), (0,)), ((), ())), preferred_element_type=jnp.float32
    ).reshape(recv, length, feat_width)
    pool_b = pool_total.astype(jnp.bfloat16)
    slot_b = slot_total.astype(jnp.bfloat16)

    if SUB_MODE == "perm":
        owned = pool_b[:img_count].astype(jnp.float32)
        for k in range(1, n_sub):
            owned = owned + lax.ppermute(
                pool_b[k * img_count : (k + 1) * img_count], "sub", shift(n_sub, -k)
            ).astype(jnp.float32)
    elif SUB_MODE == "a2a":
        back = lax.all_to_all(pool_b, "sub", split_axis=0, concat_axis=0, tiled=True).astype(jnp.float32)
        owned = jnp.sum(back.reshape(n_sub, img_count, length, feat_width), axis=0)
    else:
        owned = lax.psum_scatter(pool_b, "sub", scatter_dimension=0, tiled=True).astype(jnp.float32)

    if GRP_MODE == "perm":
        returned = jnp.concatenate(
            [slot_b[:slots]]
            + [
                lax.ppermute(slot_b[k * slots : (k + 1) * slots], "grp", shift(n_grp, -k))
                for k in range(1, n_grp)
            ],
            axis=0,
        )
    else:
        returned = lax.all_to_all(slot_b, "grp", split_axis=0, concat_axis=0, tiled=True)
    incoming_gradient = owned.reshape(img_count, length * feat_width) + jnp.dot(
        pick_onehot.T, returned.reshape(recv, length * feat_width), preferred_element_type=jnp.float32
    )
    incoming_gradient = incoming_gradient.reshape(img_count * length, feat_width)
    feature_grad = (
        inv_rms
        * (
            incoming_gradient
            - normed * jnp.mean(incoming_gradient * normed, axis=-1, keepdims=True)
        )
    ).astype(jnp.bfloat16)
    token_grad = jnp.einsum(
        "nk,dk->nd", feature_grad, proj_weight, preferred_element_type=jnp.float32
    )
    return token_grad.astype(jnp.bfloat16).reshape(img_count, length, feat_width)


def solution(mesh):
    placed = (
        P(("grp", "sub"), None, None),
        P(),
        P(("grp", "sub"), None),
        P(("grp", "sub")),
        P(("grp", "sub")),
        P(("grp", "sub")),
    )
    n_grp = mesh.shape["grp"]
    n_sub = mesh.shape["sub"]

    def run(*args):
        return local(n_grp, n_sub, *args)

    return jax.shard_map(
        run, mesh=mesh, in_specs=placed, out_specs=P(("grp", "sub"), None, None), check_vma=False
    )
```

```python
import functools

import jax
import jax.numpy as jnp
from jax import lax
from jax.experimental import pallas as pl
from jax.experimental.pallas import tpu as pltpu
from jax.sharding import PartitionSpec as P

EPSILON = 1e-05
SOFTMAX_COOLING = 0.1
SUB_MODE = "perm"
GRP_MODE = "a2a"


def normalize(tokens, proj_weight):
    image_count, length, feat_width = tokens.shape
    feature = jnp.dot(
        tokens.reshape(image_count * length, feat_width),
        proj_weight,
        preferred_element_type=jnp.float32,
    )
    inv_rms = lax.rsqrt(jnp.mean(feature * feature, axis=-1, keepdims=True) + EPSILON)
    normed = feature * inv_rms
    return (normed, inv_rms, normed.astype(jnp.bfloat16).reshape(image_count, length, feat_width))


def shift(count, step):
    return [(i, (i + step) % count) for i in range(count)]


def lane_group_sum(x, group):
    rows, width = x.shape
    xt = x.T.reshape(width // group, group, rows)
    total = jnp.sum(xt, axis=1, keepdims=True)
    return jnp.broadcast_to(total, (width // group, group, rows)).reshape(width, rows).T


def row_group_sum(x, group):
    rows, width = x.shape
    xr = x.reshape(rows // group, group, width)
    total = jnp.sum(xr, axis=1, keepdims=True)
    return jnp.broadcast_to(total, (rows // group, group, width)).reshape(rows, width)


def softmax_bwd_kernel(group, score_scale, recv, edge_at_ref, s_ref, m_ref, d_ref, g_scr):
    block = pl.program_id(0)
    firsts = s_ref.shape[0] // group

    def place(first, carry):
        row = pl.multiple_of(first * group, group)
        base = (block * firsts + first) * recv
        for second in range(recv):
            g_scr[pl.ds(row, group), second * group : (second + 1) * group] = m_ref[
                edge_at_ref[base + second]
            ].astype(jnp.float32)
        return carry

    lax.fori_loop(0, firsts, place, 0)
    expo = jnp.exp(s_ref[...])
    rows = expo / lane_group_sum(expo, group)
    cols = expo / row_group_sum(expo, group)
    grads = g_scr[...]
    d_rows = grads * cols
    d_cols = grads * rows
    d_scores = rows * (d_rows - lane_group_sum(d_rows * rows, group)) + cols * (
        d_cols - row_group_sum(d_cols * cols, group)
    )
    d_ref[...] = (d_scores * score_scale).astype(jnp.bfloat16)


def softmax_bwd(scores, edge_at, blocks, group, score_scale):
    total_rows, width = scores.shape
    recv = width // group
    block = 128 if total_rows % 128 == 0 else total_rows
    return pl.pallas_call(
        functools.partial(softmax_bwd_kernel, group, score_scale, recv),
        out_shape=jax.ShapeDtypeStruct((total_rows, width), jnp.bfloat16),
        grid_spec=pltpu.PrefetchScalarGridSpec(
            num_scalar_prefetch=1,
            grid=(total_rows // block,),
            in_specs=[
                pl.BlockSpec((block, width), lambda b, e: (b, 0)),
                pl.BlockSpec(blocks.shape, lambda b, e: (0, 0, 0)),
            ],
            out_specs=pl.BlockSpec((block, width), lambda b, e: (b, 0)),
            scratch_shapes=[pltpu.VMEM((block, width), jnp.float32)],
        ),
        compiler_params=pltpu.CompilerParams(vmem_limit_bytes=48 * 1024 * 1024),
        cost_estimate=pl.CostEstimate(
            flops=30 * total_rows * width,
            transcendentals=total_rows * width,
            bytes_accessed=6 * total_rows * width,
        ),
    )(edge_at, scores, blocks)


def local(n_grp, n_sub, tokens, proj_weight, match_grad, edge_first, pair_second_image, send_pick):
    img_count, length, feat_width = tokens.shape
    recv = send_pick.shape[0]
    slots = recv // n_grp
    group_img = img_count * n_sub
    edge_count = edge_first.shape[0]
    grp_at = lax.axis_index("grp")
    sub_at = lax.axis_index("sub")

    normed, inv_rms, normed_b = normalize(tokens, proj_weight)

    if SUB_MODE == "perm":
        pool = jnp.concatenate(
            [normed_b]
            + [
                normalize(lax.ppermute(tokens, "sub", shift(n_sub, k)), proj_weight)[2]
                for k in range(1, n_sub)
            ],
            axis=0,
        )
        first_at = ((sub_at - edge_first // img_count) % n_sub) * img_count + edge_first % img_count
    elif SUB_MODE == "gather":
        pool = lax.all_gather(normed_b, "sub", axis=0, tiled=True)
        first_at = edge_first
    else:
        pool = lax.all_to_all(
            jnp.concatenate([normed_b] * n_sub, axis=0), "sub", split_axis=0, concat_axis=0, tiled=True
        )
        first_at = edge_first

    picks = send_pick.reshape(n_grp, slots)
    if GRP_MODE == "perm":
        order = picks[(grp_at + jnp.arange(n_grp, dtype=jnp.int32)) % n_grp].reshape(recv)
    else:
        order = send_pick
    outgoing = jnp.broadcast_to(tokens[img_count - 1], (recv, length, feat_width))
    for image in range(img_count - 2, -1, -1):
        outgoing = jnp.where(order[:, None, None] == image, tokens[image], outgoing)
    if GRP_MODE == "perm":
        received = jnp.concatenate(
            [outgoing[:slots]]
            + [
                lax.ppermute(outgoing[k * slots : (k + 1) * slots], "grp", shift(n_grp, k))
                for k in range(1, n_grp)
            ],
            axis=0,
        )
        second_at = ((grp_at - pair_second_image // slots) % n_grp) * slots + pair_second_image % slots
    else:
        received = normalize(
            lax.all_to_all(outgoing, "grp", split_axis=0, concat_axis=0, tiled=True), proj_weight
        )[2]
        second_at = pair_second_image

    pair_at = first_at * recv + second_at
    edge_ids = jnp.arange(edge_count, dtype=jnp.int32)
    edge_at = jnp.min(
        jnp.where(
            lax.broadcasted_iota(jnp.int32, (group_img * recv, edge_count), 0) == pair_at[None, :],
            edge_ids[None, :],
            edge_count,
        ),
        axis=1,
    )
    blocks = jnp.concatenate(
        [match_grad.reshape(edge_count, length, length), jnp.zeros((1, length, length), match_grad.dtype)],
        axis=0,
    )
    pool2 = pool.reshape(group_img * length, feat_width)
    recv2 = received.reshape(recv * length, feat_width)
    score_scale = 1.0 / (feat_width * SOFTMAX_COOLING)
    scores = (
        lax.dot_general(pool2, recv2, (((1,), (1,)), ((), ())), preferred_element_type=jnp.float32)
        * score_scale
    )
    d_scaled = softmax_bwd(scores, edge_at, blocks, length, score_scale)
    pool_total = jnp.dot(d_scaled, recv2, preferred_element_type=jnp.float32).reshape(
        group_img, length, feat_width
    )
    slot_total = lax.dot_general(
        d_scaled, pool2, (((0,), (0,)), ((), ())), preferred_element_type=jnp.float32
    ).reshape(recv, length, feat_width)
    pool_b = pool_total.astype(jnp.bfloat16)
    slot_b = slot_total.astype(jnp.bfloat16)

    if SUB_MODE == "perm":
        owned = pool_b[:img_count].astype(jnp.float32)
        for k in range(1, n_sub):
            owned = owned + lax.ppermute(
                pool_b[k * img_count : (k + 1) * img_count], "sub", shift(n_sub, -k)
            ).astype(jnp.float32)
    elif SUB_MODE == "a2a":
        back = lax.all_to_all(pool_b, "sub", split_axis=0, concat_axis=0, tiled=True).astype(jnp.float32)
        owned = jnp.sum(back.reshape(n_sub, img_count, length, feat_width), axis=0)
    else:
        owned = lax.psum_scatter(pool_b, "sub", scatter_dimension=0, tiled=True).astype(jnp.float32)

    if GRP_MODE == "perm":
        returned = jnp.concatenate(
            [slot_b[:slots]]
            + [
                lax.ppermute(slot_b[k * slots : (k + 1) * slots], "grp", shift(n_grp, -k))
                for k in range(1, n_grp)
            ],
            axis=0,
        )
    else:
        returned = lax.all_to_all(slot_b, "grp", split_axis=0, concat_axis=0, tiled=True)
    slot_images = order[:, None, None, None] == jnp.arange(img_count, dtype=jnp.int32)[None, :, None, None]
    incoming_gradient = owned + jnp.sum(
        jnp.where(slot_images, returned.astype(jnp.float32)[:, None], 0.0), axis=0
    )
    incoming_gradient = incoming_gradient.reshape(img_count * length, feat_width)
    feature_grad = (
        inv_rms
        * (
            incoming_gradient
            - normed * jnp.mean(incoming_gradient * normed, axis=-1, keepdims=True)
        )
    ).astype(jnp.bfloat16)
    token_grad = jnp.einsum(
        "nk,dk->nd", feature_grad, proj_weight, preferred_element_type=jnp.float32
    )
    return token_grad.astype(jnp.bfloat16).reshape(img_count, length, feat_width)


def solution(mesh):
    placed = (
        P(("grp", "sub"), None, None),
        P(),
        P(("grp", "sub"), None),
        P(("grp", "sub")),
        P(("grp", "sub")),
        P(("grp", "sub")),
    )
    n_grp = mesh.shape["grp"]
    n_sub = mesh.shape["sub"]

    def run(*args):
        return local(n_grp, n_sub, *args)

    return jax.shard_map(
        run, mesh=mesh, in_specs=placed, out_specs=P(("grp", "sub"), None, None), check_vma=False
    )
```

```python
import functools

import jax
import jax.numpy as jnp
from jax import lax
from jax.experimental import pallas as pl
from jax.experimental.pallas import tpu as pltpu
from jax.sharding import PartitionSpec as P

EPSILON = 1e-05
SOFTMAX_COOLING = 0.1
SUB_MODE = "perm"
GRP_MODE = "a2a"


def normalize(tokens, proj_weight):
    image_count, length, feat_width = tokens.shape
    feature = jnp.dot(
        tokens.reshape(image_count * length, feat_width),
        proj_weight,
        preferred_element_type=jnp.float32,
    )
    inv_rms = lax.rsqrt(jnp.mean(feature * feature, axis=-1, keepdims=True) + EPSILON)
    normed = feature * inv_rms
    return (normed, inv_rms, normed.astype(jnp.bfloat16).reshape(image_count, length, feat_width))


def shift(count, step):
    return [(i, (i + step) % count) for i in range(count)]


def lane_group_sum(x, group):
    rows, width = x.shape
    xt = x.T.reshape(width // group, group, rows)
    total = jnp.sum(xt, axis=1, keepdims=True)
    return jnp.broadcast_to(total, (width // group, group, rows)).reshape(width, rows).T


def row_group_sum(x, group):
    rows, width = x.shape
    xr = x.reshape(rows // group, group, width)
    total = jnp.sum(xr, axis=1, keepdims=True)
    return jnp.broadcast_to(total, (rows // group, group, width)).reshape(rows, width)


def place_kernel(group, recv, edge_at_ref, m_ref, g_ref):
    block = pl.program_id(0)
    firsts = g_ref.shape[0] // group

    def place(first, carry):
        row = pl.multiple_of(first * group, group)
        base = (block * firsts + first) * recv
        for second in range(recv):
            g_ref[pl.ds(row, group), second * group : (second + 1) * group] = m_ref[
                edge_at_ref[base + second]
            ]
        return carry

    lax.fori_loop(0, firsts, place, 0)


def place_grads(edge_at, blocks, total_rows, width, group):
    recv = width // group
    block = 128 if total_rows % 128 == 0 else total_rows
    return pl.pallas_call(
        functools.partial(place_kernel, group, recv),
        out_shape=jax.ShapeDtypeStruct((total_rows, width), blocks.dtype),
        grid_spec=pltpu.PrefetchScalarGridSpec(
            num_scalar_prefetch=1,
            grid=(total_rows // block,),
            in_specs=[pl.BlockSpec(blocks.shape, lambda b, e: (0, 0, 0))],
            out_specs=pl.BlockSpec((block, width), lambda b, e: (b, 0)),
        ),
        compiler_params=pltpu.CompilerParams(vmem_limit_bytes=32 * 1024 * 1024),
        cost_estimate=pl.CostEstimate(
            flops=0, transcendentals=0, bytes_accessed=2 * total_rows * width + 2 * blocks.size
        ),
    )(edge_at, blocks)


def softmax_bwd_kernel(group, score_scale, s_ref, g_ref, d_ref):
    expo = jnp.exp(s_ref[...])
    rows = expo / lane_group_sum(expo, group)
    cols = expo / row_group_sum(expo, group)
    grads = g_ref[...].astype(jnp.float32)
    d_rows = grads * cols
    d_cols = grads * rows
    d_scores = rows * (d_rows - lane_group_sum(d_rows * rows, group)) + cols * (
        d_cols - row_group_sum(d_cols * cols, group)
    )
    d_ref[...] = (d_scores * score_scale).astype(jnp.bfloat16)


def softmax_bwd(scores, grads, group, score_scale):
    total_rows, width = scores.shape
    block = 128 if total_rows % 128 == 0 else total_rows
    return pl.pallas_call(
        functools.partial(softmax_bwd_kernel, group, score_scale),
        out_shape=jax.ShapeDtypeStruct((total_rows, width), jnp.bfloat16),
        grid=(total_rows // block,),
        in_specs=[
            pl.BlockSpec((block, width), lambda b: (b, 0)),
            pl.BlockSpec((block, width), lambda b: (b, 0)),
        ],
        out_specs=pl.BlockSpec((block, width), lambda b: (b, 0)),
        compiler_params=pltpu.CompilerParams(vmem_limit_bytes=48 * 1024 * 1024),
        cost_estimate=pl.CostEstimate(
            flops=30 * total_rows * width,
            transcendentals=total_rows * width,
            bytes_accessed=8 * total_rows * width,
        ),
    )(scores, grads)


def local(n_grp, n_sub, tokens, proj_weight, match_grad, edge_first, pair_second_image, send_pick):
    img_count, length, feat_width = tokens.shape
    recv = send_pick.shape[0]
    slots = recv // n_grp
    group_img = img_count * n_sub
    edge_count = edge_first.shape[0]
    grp_at = lax.axis_index("grp")
    sub_at = lax.axis_index("sub")

    normed, inv_rms, normed_b = normalize(tokens, proj_weight)

    if SUB_MODE == "perm":
        pool = jnp.concatenate(
            [normed_b]
            + [
                normalize(lax.ppermute(tokens, "sub", shift(n_sub, k)), proj_weight)[2]
                for k in range(1, n_sub)
            ],
            axis=0,
        )
        first_at = ((sub_at - edge_first // img_count) % n_sub) * img_count + edge_first % img_count
    elif SUB_MODE == "gather":
        pool = lax.all_gather(normed_b, "sub", axis=0, tiled=True)
        first_at = edge_first
    else:
        pool = lax.all_to_all(
            jnp.concatenate([normed_b] * n_sub, axis=0), "sub", split_axis=0, concat_axis=0, tiled=True
        )
        first_at = edge_first

    picks = send_pick.reshape(n_grp, slots)
    if GRP_MODE == "perm":
        order = picks[(grp_at + jnp.arange(n_grp, dtype=jnp.int32)) % n_grp].reshape(recv)
    else:
        order = send_pick
    outgoing = jnp.broadcast_to(tokens[img_count - 1], (recv, length, feat_width))
    for image in range(img_count - 2, -1, -1):
        outgoing = jnp.where(order[:, None, None] == image, tokens[image], outgoing)
    if GRP_MODE == "perm":
        received = jnp.concatenate(
            [outgoing[:slots]]
            + [
                lax.ppermute(outgoing[k * slots : (k + 1) * slots], "grp", shift(n_grp, k))
                for k in range(1, n_grp)
            ],
            axis=0,
        )
        second_at = ((grp_at - pair_second_image // slots) % n_grp) * slots + pair_second_image % slots
    else:
        received = normalize(
            lax.all_to_all(outgoing, "grp", split_axis=0, concat_axis=0, tiled=True), proj_weight
        )[2]
        second_at = pair_second_image

    pair_at = first_at * recv + second_at
    edge_ids = jnp.arange(edge_count, dtype=jnp.int32)
    edge_at = jnp.min(
        jnp.where(
            lax.broadcasted_iota(jnp.int32, (group_img * recv, edge_count), 0) == pair_at[None, :],
            edge_ids[None, :],
            edge_count,
        ),
        axis=1,
    )
    blocks = jnp.concatenate(
        [match_grad.reshape(edge_count, length, length), jnp.zeros((1, length, length), match_grad.dtype)],
        axis=0,
    )
    grads = place_grads(edge_at, blocks, group_img * length, recv * length, length)
    pool2 = pool.reshape(group_img * length, feat_width)
    recv2 = received.reshape(recv * length, feat_width)
    score_scale = 1.0 / (feat_width * SOFTMAX_COOLING)
    scores = (
        lax.dot_general(pool2, recv2, (((1,), (1,)), ((), ())), preferred_element_type=jnp.float32)
        * score_scale
    )
    d_scaled = softmax_bwd(scores, grads, length, score_scale)
    pool_total = jnp.dot(d_scaled, recv2, preferred_element_type=jnp.float32).reshape(
        group_img, length, feat_width
    )
    slot_total = lax.dot_general(
        d_scaled, pool2, (((0,), (0,)), ((), ())), preferred_element_type=jnp.float32
    ).reshape(recv, length, feat_width)
    pool_b = pool_total.astype(jnp.bfloat16)
    slot_b = slot_total.astype(jnp.bfloat16)

    if SUB_MODE == "perm":
        owned = pool_b[:img_count].astype(jnp.float32)
        for k in range(1, n_sub):
            owned = owned + lax.ppermute(
                pool_b[k * img_count : (k + 1) * img_count], "sub", shift(n_sub, -k)
            ).astype(jnp.float32)
    elif SUB_MODE == "a2a":
        back = lax.all_to_all(pool_b, "sub", split_axis=0, concat_axis=0, tiled=True).astype(jnp.float32)
        owned = jnp.sum(back.reshape(n_sub, img_count, length, feat_width), axis=0)
    else:
        owned = lax.psum_scatter(pool_b, "sub", scatter_dimension=0, tiled=True).astype(jnp.float32)

    if GRP_MODE == "perm":
        returned = jnp.concatenate(
            [slot_b[:slots]]
            + [
                lax.ppermute(slot_b[k * slots : (k + 1) * slots], "grp", shift(n_grp, -k))
                for k in range(1, n_grp)
            ],
            axis=0,
        )
    else:
        returned = lax.all_to_all(slot_b, "grp", split_axis=0, concat_axis=0, tiled=True)
    slot_images = order[:, None, None, None] == jnp.arange(img_count, dtype=jnp.int32)[None, :, None, None]
    incoming_gradient = owned + jnp.sum(
        jnp.where(slot_images, returned.astype(jnp.float32)[:, None], 0.0), axis=0
    )
    incoming_gradient = incoming_gradient.reshape(img_count * length, feat_width)
    feature_grad = (
        inv_rms
        * (
            incoming_gradient
            - normed * jnp.mean(incoming_gradient * normed, axis=-1, keepdims=True)
        )
    ).astype(jnp.bfloat16)
    token_grad = jnp.einsum(
        "nk,dk->nd", feature_grad, proj_weight, preferred_element_type=jnp.float32
    )
    return token_grad.astype(jnp.bfloat16).reshape(img_count, length, feat_width)


def solution(mesh):
    placed = (
        P(("grp", "sub"), None, None),
        P(),
        P(("grp", "sub"), None),
        P(("grp", "sub")),
        P(("grp", "sub")),
        P(("grp", "sub")),
    )
    n_grp = mesh.shape["grp"]
    n_sub = mesh.shape["sub"]

    def run(*args):
        return local(n_grp, n_sub, *args)

    return jax.shard_map(
        run, mesh=mesh, in_specs=placed, out_specs=P(("grp", "sub"), None, None), check_vma=False
    )
```

```python
import functools

import jax
import jax.numpy as jnp
from jax import lax
from jax.experimental import pallas as pl
from jax.experimental.pallas import tpu as pltpu
from jax.sharding import PartitionSpec as P

EPSILON = 1e-05
SOFTMAX_COOLING = 0.1
SUB_MODE = "perm"


def normalize(tokens, proj_weight):
    image_count, length, feat_width = tokens.shape
    feature = jnp.dot(
        tokens.reshape(image_count * length, feat_width),
        proj_weight,
        preferred_element_type=jnp.float32,
    )
    inv_rms = lax.rsqrt(jnp.mean(feature * feature, axis=-1, keepdims=True) + EPSILON)
    normed = feature * inv_rms
    return (normed, inv_rms, normed.astype(jnp.bfloat16).reshape(image_count, length, feat_width))


def shift(count, step):
    return [(i, (i + step) % count) for i in range(count)]


def lane_group_sum(x, group):
    rows, width = x.shape
    xt = x.T.reshape(width // group, group, rows)
    total = jnp.sum(xt, axis=1, keepdims=True)
    return jnp.broadcast_to(total, (width // group, group, rows)).reshape(width, rows).T


def row_group_sum(x, group):
    rows, width = x.shape
    xr = x.reshape(rows // group, group, width)
    total = jnp.sum(xr, axis=1, keepdims=True)
    return jnp.broadcast_to(total, (rows // group, group, width)).reshape(rows, width)


def place_kernel(group, recv, edge_at_ref, m_ref, g_ref):
    block = pl.program_id(0)
    firsts = g_ref.shape[0] // group

    def place(first, carry):
        row = pl.multiple_of(first * group, group)
        base = (block * firsts + first) * recv
        for second in range(recv):
            g_ref[pl.ds(row, group), second * group : (second + 1) * group] = m_ref[
                edge_at_ref[base + second]
            ]
        return carry

    lax.fori_loop(0, firsts, place, 0)


def place_grads(edge_at, blocks, total_rows, width, group):
    recv = width // group
    block = 128 if total_rows % 128 == 0 else total_rows
    return pl.pallas_call(
        functools.partial(place_kernel, group, recv),
        out_shape=jax.ShapeDtypeStruct((total_rows, width), blocks.dtype),
        grid_spec=pltpu.PrefetchScalarGridSpec(
            num_scalar_prefetch=1,
            grid=(total_rows // block,),
            in_specs=[pl.BlockSpec(blocks.shape, lambda b, e: (0, 0, 0))],
            out_specs=pl.BlockSpec((block, width), lambda b, e: (b, 0)),
        ),
        compiler_params=pltpu.CompilerParams(vmem_limit_bytes=32 * 1024 * 1024),
        cost_estimate=pl.CostEstimate(
            flops=0, transcendentals=0, bytes_accessed=2 * total_rows * width + 2 * blocks.size
        ),
    )(edge_at, blocks)


def softmax_bwd_kernel(group, score_scale, s_ref, g_ref, d_ref):
    expo = jnp.exp(s_ref[...])
    rows = expo / lane_group_sum(expo, group)
    cols = expo / row_group_sum(expo, group)
    grads = g_ref[...].astype(jnp.float32)
    d_rows = grads * cols
    d_cols = grads * rows
    d_scores = rows * (d_rows - lane_group_sum(d_rows * rows, group)) + cols * (
        d_cols - row_group_sum(d_cols * cols, group)
    )
    d_ref[...] = (d_scores * score_scale).astype(jnp.bfloat16)


def softmax_bwd(scores, grads, group, score_scale):
    total_rows, width = scores.shape
    block = 128 if total_rows % 128 == 0 else total_rows
    return pl.pallas_call(
        functools.partial(softmax_bwd_kernel, group, score_scale),
        out_shape=jax.ShapeDtypeStruct((total_rows, width), jnp.bfloat16),
        grid=(total_rows // block,),
        in_specs=[
            pl.BlockSpec((block, width), lambda b: (b, 0)),
            pl.BlockSpec((block, width), lambda b: (b, 0)),
        ],
        out_specs=pl.BlockSpec((block, width), lambda b: (b, 0)),
        compiler_params=pltpu.CompilerParams(vmem_limit_bytes=48 * 1024 * 1024),
        cost_estimate=pl.CostEstimate(
            flops=30 * total_rows * width,
            transcendentals=total_rows * width,
            bytes_accessed=8 * total_rows * width,
        ),
    )(scores, grads)


def local(n_grp, n_sub, tokens, proj_weight, match_grad, edge_first, pair_second_image, send_pick):
    img_count, length, feat_width = tokens.shape
    recv = send_pick.shape[0]
    slots = recv // n_grp
    group_img = img_count * n_sub
    edge_count = edge_first.shape[0]
    grp_at = lax.axis_index("grp")
    sub_at = lax.axis_index("sub")

    normed, inv_rms, normed_b = normalize(tokens, proj_weight)

    if SUB_MODE == "perm":
        pool = jnp.concatenate(
            [normed_b]
            + [
                normalize(lax.ppermute(tokens, "sub", shift(n_sub, k)), proj_weight)[2]
                for k in range(1, n_sub)
            ],
            axis=0,
        )
        first_at = ((sub_at - edge_first // img_count) % n_sub) * img_count + edge_first % img_count
    elif SUB_MODE == "gather":
        pool = lax.all_gather(normed_b, "sub", axis=0, tiled=True)
        first_at = edge_first
    else:
        pool = lax.all_to_all(
            jnp.concatenate([normed_b] * n_sub, axis=0), "sub", split_axis=0, concat_axis=0, tiled=True
        )
        first_at = edge_first

    picks = send_pick.reshape(n_grp, slots)
    whole = slots == img_count
    if whole:
        pick_rows = jnp.pad(
            picks.astype(tokens.dtype)[:, None, :], ((0, 0), (0, 15), (0, feat_width - slots))
        )
        outgoing = jnp.concatenate(
            [jnp.broadcast_to(tokens.reshape(1, img_count * length, feat_width), (n_grp, img_count * length, feat_width)), pick_rows],
            axis=1,
        )
        arrived = lax.all_to_all(outgoing, "grp", split_axis=0, concat_axis=0, tiled=True)
        received = normalize(
            arrived[:, : img_count * length].reshape(n_grp * img_count, length, feat_width), proj_weight
        )[2]
        got_picks = arrived[:, img_count * length, :slots].astype(jnp.int32).reshape(recv)
        second_at = (pair_second_image // slots) * img_count + jnp.take(got_picks, pair_second_image)
    else:
        outgoing = jnp.broadcast_to(tokens[img_count - 1], (recv, length, feat_width))
        for image in range(img_count - 2, -1, -1):
            outgoing = jnp.where(send_pick[:, None, None] == image, tokens[image], outgoing)
        received = normalize(
            lax.all_to_all(outgoing, "grp", split_axis=0, concat_axis=0, tiled=True), proj_weight
        )[2]
        second_at = pair_second_image

    pair_at = first_at * recv + second_at
    edge_ids = jnp.arange(edge_count, dtype=jnp.int32)
    edge_at = jnp.min(
        jnp.where(
            lax.broadcasted_iota(jnp.int32, (group_img * recv, edge_count), 0) == pair_at[None, :],
            edge_ids[None, :],
            edge_count,
        ),
        axis=1,
    )
    blocks = jnp.concatenate(
        [match_grad.reshape(edge_count, length, length), jnp.zeros((1, length, length), match_grad.dtype)],
        axis=0,
    )
    grads = place_grads(edge_at, blocks, group_img * length, recv * length, length)
    pool2 = pool.reshape(group_img * length, feat_width)
    recv2 = received.reshape(recv * length, feat_width)
    score_scale = 1.0 / (feat_width * SOFTMAX_COOLING)
    scores = (
        lax.dot_general(pool2, recv2, (((1,), (1,)), ((), ())), preferred_element_type=jnp.float32)
        * score_scale
    )
    d_scaled = softmax_bwd(scores, grads, length, score_scale)
    pool_total = jnp.dot(d_scaled, recv2, preferred_element_type=jnp.float32).reshape(
        group_img, length, feat_width
    )
    slot_total = lax.dot_general(
        d_scaled, pool2, (((0,), (0,)), ((), ())), preferred_element_type=jnp.float32
    ).reshape(recv, length, feat_width)
    pool_b = pool_total.astype(jnp.bfloat16)
    slot_b = slot_total.astype(jnp.bfloat16)

    if SUB_MODE == "perm":
        owned = pool_b[:img_count].astype(jnp.float32)
        for k in range(1, n_sub):
            owned = owned + lax.ppermute(
                pool_b[k * img_count : (k + 1) * img_count], "sub", shift(n_sub, -k)
            ).astype(jnp.float32)
    elif SUB_MODE == "a2a":
        back = lax.all_to_all(pool_b, "sub", split_axis=0, concat_axis=0, tiled=True).astype(jnp.float32)
        owned = jnp.sum(back.reshape(n_sub, img_count, length, feat_width), axis=0)
    else:
        owned = lax.psum_scatter(pool_b, "sub", scatter_dimension=0, tiled=True).astype(jnp.float32)

    returned = lax.all_to_all(slot_b, "grp", split_axis=0, concat_axis=0, tiled=True).astype(jnp.float32)
    if whole:
        incoming_gradient = owned + jnp.sum(returned.reshape(n_grp, img_count, length, feat_width), axis=0)
    else:
        slot_images = send_pick[:, None, None, None] == jnp.arange(img_count, dtype=jnp.int32)[None, :, None, None]
        incoming_gradient = owned + jnp.sum(jnp.where(slot_images, returned[:, None], 0.0), axis=0)
    incoming_gradient = incoming_gradient.reshape(img_count * length, feat_width)
    feature_grad = (
        inv_rms
        * (
            incoming_gradient
            - normed * jnp.mean(incoming_gradient * normed, axis=-1, keepdims=True)
        )
    ).astype(jnp.bfloat16)
    token_grad = jnp.einsum(
        "nk,dk->nd", feature_grad, proj_weight, preferred_element_type=jnp.float32
    )
    return token_grad.astype(jnp.bfloat16).reshape(img_count, length, feat_width)


def solution(mesh):
    placed = (
        P(("grp", "sub"), None, None),
        P(),
        P(("grp", "sub"), None),
        P(("grp", "sub")),
        P(("grp", "sub")),
        P(("grp", "sub")),
    )
    n_grp = mesh.shape["grp"]
    n_sub = mesh.shape["sub"]

    def run(*args):
        return local(n_grp, n_sub, *args)

    return jax.shard_map(
        run, mesh=mesh, in_specs=placed, out_specs=P(("grp", "sub"), None, None), check_vma=False
    )
```

```python
import functools

import jax
import jax.numpy as jnp
from jax import lax
from jax.experimental import pallas as pl
from jax.experimental.pallas import tpu as pltpu
from jax.sharding import PartitionSpec as P

EPSILON = 1e-05
SOFTMAX_COOLING = 0.1
SUB_MODE = "perm"
GRP_MODE = "a2a"


def normalize(tokens, proj_weight):
    image_count, length, feat_width = tokens.shape
    feature = jnp.dot(
        tokens.reshape(image_count * length, feat_width),
        proj_weight,
        preferred_element_type=jnp.float32,
    )
    inv_rms = lax.rsqrt(jnp.mean(feature * feature, axis=-1, keepdims=True) + EPSILON)
    normed = feature * inv_rms
    return (normed, inv_rms, normed.astype(jnp.bfloat16).reshape(image_count, length, feat_width))


def shift(count, step):
    return [(i, (i + step) % count) for i in range(count)]


def lane_group_sum(x, group):
    rows, width = x.shape
    xt = x.T.reshape(width // group, group, rows)
    total = jnp.sum(xt, axis=1, keepdims=True)
    return jnp.broadcast_to(total, (width // group, group, rows)).reshape(width, rows).T


def row_group_sum(x, group):
    rows, width = x.shape
    xr = x.reshape(rows // group, group, width)
    total = jnp.sum(xr, axis=1, keepdims=True)
    return jnp.broadcast_to(total, (rows // group, group, width)).reshape(rows, width)


def place_kernel(group, recv, edge_at_ref, m_ref, g_ref):
    block = pl.program_id(0)
    firsts = g_ref.shape[0] // group

    def place(first, carry):
        row = pl.multiple_of(first * group, group)
        base = (block * firsts + first) * recv
        for second in range(recv):
            g_ref[pl.ds(row, group), second * group : (second + 1) * group] = m_ref[
                edge_at_ref[base + second]
            ]
        return carry

    lax.fori_loop(0, firsts, place, 0)


def place_grads(edge_at, blocks, total_rows, width, group):
    recv = width // group
    block = 128 if total_rows % 128 == 0 else total_rows
    return pl.pallas_call(
        functools.partial(place_kernel, group, recv),
        out_shape=jax.ShapeDtypeStruct((total_rows, width), blocks.dtype),
        grid_spec=pltpu.PrefetchScalarGridSpec(
            num_scalar_prefetch=1,
            grid=(total_rows // block,),
            in_specs=[pl.BlockSpec(blocks.shape, lambda b, e: (0, 0, 0))],
            out_specs=pl.BlockSpec((block, width), lambda b, e: (b, 0)),
        ),
        compiler_params=pltpu.CompilerParams(vmem_limit_bytes=32 * 1024 * 1024),
        cost_estimate=pl.CostEstimate(
            flops=0, transcendentals=0, bytes_accessed=2 * total_rows * width + 2 * blocks.size
        ),
    )(edge_at, blocks)


def softmax_bwd_kernel(group, score_scale, p_ref, r_ref, g_ref, pool_ref, slot_ref, slot_acc):
    step = pl.program_id(0)
    first_feats = p_ref[...]
    second_feats = r_ref[...]
    scores = (
        lax.dot_general(
            first_feats, second_feats, (((1,), (1,)), ((), ())), preferred_element_type=jnp.float32
        )
        * score_scale
    )
    expo = jnp.exp(scores)
    rows = expo / lane_group_sum(expo, group)
    cols = expo / row_group_sum(expo, group)
    grads = g_ref[...].astype(jnp.float32)
    d_rows = grads * cols
    d_cols = grads * rows
    d_scores = rows * (d_rows - lane_group_sum(d_rows * rows, group)) + cols * (
        d_cols - row_group_sum(d_cols * cols, group)
    )
    d_scaled = d_scores * score_scale
    pool_ref[...] = jnp.dot(
        d_scaled.astype(jnp.bfloat16), second_feats, preferred_element_type=jnp.float32
    ).astype(pool_ref.dtype)
    slot_step = jnp.dot(
        d_scaled.T.astype(jnp.bfloat16), first_feats, preferred_element_type=jnp.float32
    )

    @pl.when(step == 0)
    def _():
        slot_acc[...] = slot_step

    @pl.when(step > 0)
    def _():
        slot_acc[...] += slot_step

    @pl.when(step == pl.num_programs(0) - 1)
    def _():
        slot_ref[...] = slot_acc[...].astype(slot_ref.dtype)


def softmax_bwd(pool2, recv2, grads, group, score_scale):
    total_rows, width = grads.shape
    feat_width = pool2.shape[1]
    block = 128 if total_rows % 128 == 0 else total_rows
    return pl.pallas_call(
        functools.partial(softmax_bwd_kernel, group, score_scale),
        out_shape=(
            jax.ShapeDtypeStruct((total_rows, feat_width), jnp.bfloat16),
            jax.ShapeDtypeStruct((width, feat_width), jnp.bfloat16),
        ),
        grid=(total_rows // block,),
        in_specs=[
            pl.BlockSpec((block, feat_width), lambda b: (b, 0)),
            pl.BlockSpec((width, feat_width), lambda b: (0, 0)),
            pl.BlockSpec((block, width), lambda b: (b, 0)),
        ],
        out_specs=(
            pl.BlockSpec((block, feat_width), lambda b: (b, 0)),
            pl.BlockSpec((width, feat_width), lambda b: (0, 0)),
        ),
        scratch_shapes=[pltpu.VMEM((width, feat_width), jnp.float32)],
        compiler_params=pltpu.CompilerParams(vmem_limit_bytes=48 * 1024 * 1024),
        cost_estimate=pl.CostEstimate(
            flops=30 * total_rows * width + 6 * total_rows * width * feat_width,
            transcendentals=total_rows * width,
            bytes_accessed=2 * total_rows * width + 2 * (total_rows + width) * feat_width,
        ),
    )(pool2, recv2, grads)


def local(n_grp, n_sub, tokens, proj_weight, match_grad, edge_first, pair_second_image, send_pick):
    img_count, length, feat_width = tokens.shape
    recv = send_pick.shape[0]
    slots = recv // n_grp
    group_img = img_count * n_sub
    edge_count = edge_first.shape[0]
    grp_at = lax.axis_index("grp")
    sub_at = lax.axis_index("sub")

    normed, inv_rms, normed_b = normalize(tokens, proj_weight)

    if SUB_MODE == "perm":
        pool = jnp.concatenate(
            [normed_b]
            + [
                normalize(lax.ppermute(tokens, "sub", shift(n_sub, k)), proj_weight)[2]
                for k in range(1, n_sub)
            ],
            axis=0,
        )
        first_at = ((sub_at - edge_first // img_count) % n_sub) * img_count + edge_first % img_count
    elif SUB_MODE == "gather":
        pool = lax.all_gather(normed_b, "sub", axis=0, tiled=True)
        first_at = edge_first
    else:
        pool = lax.all_to_all(
            jnp.concatenate([normed_b] * n_sub, axis=0), "sub", split_axis=0, concat_axis=0, tiled=True
        )
        first_at = edge_first

    picks = send_pick.reshape(n_grp, slots)
    if GRP_MODE == "perm":
        order = picks[(grp_at + jnp.arange(n_grp, dtype=jnp.int32)) % n_grp].reshape(recv)
    else:
        order = send_pick
    outgoing = jnp.broadcast_to(tokens[img_count - 1], (recv, length, feat_width))
    for image in range(img_count - 2, -1, -1):
        outgoing = jnp.where(order[:, None, None] == image, tokens[image], outgoing)
    if GRP_MODE == "perm":
        received = jnp.concatenate(
            [outgoing[:slots]]
            + [
                lax.ppermute(outgoing[k * slots : (k + 1) * slots], "grp", shift(n_grp, k))
                for k in range(1, n_grp)
            ],
            axis=0,
        )
        second_at = ((grp_at - pair_second_image // slots) % n_grp) * slots + pair_second_image % slots
    else:
        received = normalize(
            lax.all_to_all(outgoing, "grp", split_axis=0, concat_axis=0, tiled=True), proj_weight
        )[2]
        second_at = pair_second_image

    pair_at = first_at * recv + second_at
    edge_ids = jnp.arange(edge_count, dtype=jnp.int32)
    edge_at = jnp.min(
        jnp.where(
            lax.broadcasted_iota(jnp.int32, (group_img * recv, edge_count), 0) == pair_at[None, :],
            edge_ids[None, :],
            edge_count,
        ),
        axis=1,
    )
    blocks = jnp.concatenate(
        [match_grad.reshape(edge_count, length, length), jnp.zeros((1, length, length), match_grad.dtype)],
        axis=0,
    )
    grads = place_grads(edge_at, blocks, group_img * length, recv * length, length)
    pool2 = pool.reshape(group_img * length, feat_width)
    recv2 = received.reshape(recv * length, feat_width)
    score_scale = 1.0 / (feat_width * SOFTMAX_COOLING)
    pool_b, slot_b = softmax_bwd(pool2, recv2, grads, length, score_scale)
    pool_b = pool_b.reshape(group_img, length, feat_width)
    slot_b = slot_b.reshape(recv, length, feat_width)

    if SUB_MODE == "perm":
        owned = pool_b[:img_count].astype(jnp.float32)
        for k in range(1, n_sub):
            owned = owned + lax.ppermute(
                pool_b[k * img_count : (k + 1) * img_count], "sub", shift(n_sub, -k)
            ).astype(jnp.float32)
    elif SUB_MODE == "a2a":
        back = lax.all_to_all(pool_b, "sub", split_axis=0, concat_axis=0, tiled=True).astype(jnp.float32)
        owned = jnp.sum(back.reshape(n_sub, img_count, length, feat_width), axis=0)
    else:
        owned = lax.psum_scatter(pool_b, "sub", scatter_dimension=0, tiled=True).astype(jnp.float32)

    if GRP_MODE == "perm":
        returned = jnp.concatenate(
            [slot_b[:slots]]
            + [
                lax.ppermute(slot_b[k * slots : (k + 1) * slots], "grp", shift(n_grp, -k))
                for k in range(1, n_grp)
            ],
            axis=0,
        )
    else:
        returned = lax.all_to_all(slot_b, "grp", split_axis=0, concat_axis=0, tiled=True)
    slot_images = order[:, None, None, None] == jnp.arange(img_count, dtype=jnp.int32)[None, :, None, None]
    incoming_gradient = owned + jnp.sum(
        jnp.where(slot_images, returned.astype(jnp.float32)[:, None], 0.0), axis=0
    )
    incoming_gradient = incoming_gradient.reshape(img_count * length, feat_width)
    feature_grad = (
        inv_rms
        * (
            incoming_gradient
            - normed * jnp.mean(incoming_gradient * normed, axis=-1, keepdims=True)
        )
    ).astype(jnp.bfloat16)
    token_grad = jnp.einsum(
        "nk,dk->nd", feature_grad, proj_weight, preferred_element_type=jnp.float32
    )
    return token_grad.astype(jnp.bfloat16).reshape(img_count, length, feat_width)


def solution(mesh):
    placed = (
        P(("grp", "sub"), None, None),
        P(),
        P(("grp", "sub"), None),
        P(("grp", "sub")),
        P(("grp", "sub")),
        P(("grp", "sub")),
    )
    n_grp = mesh.shape["grp"]
    n_sub = mesh.shape["sub"]

    def run(*args):
        return local(n_grp, n_sub, *args)

    return jax.shard_map(
        run, mesh=mesh, in_specs=placed, out_specs=P(("grp", "sub"), None, None), check_vma=False
    )
```

```python
import functools

import jax
import jax.numpy as jnp
from jax import lax
from jax.experimental import pallas as pl
from jax.experimental.pallas import tpu as pltpu
from jax.sharding import PartitionSpec as P

EPSILON = 1e-05
SOFTMAX_COOLING = 0.1
SUB_MODE = "perm"
GRP_MODE = "a2a"


def normalize(tokens, proj_weight):
    image_count, length, feat_width = tokens.shape
    feature = jnp.dot(
        tokens.reshape(image_count * length, feat_width),
        proj_weight,
        preferred_element_type=jnp.float32,
    )
    inv_rms = lax.rsqrt(jnp.mean(feature * feature, axis=-1, keepdims=True) + EPSILON)
    normed = feature * inv_rms
    return (normed, inv_rms, normed.astype(jnp.bfloat16).reshape(image_count, length, feat_width))


def shift(count, step):
    return [(i, (i + step) % count) for i in range(count)]


def lane_group_sum(x, group):
    rows, width = x.shape
    xt = x.T.reshape(width // group, group, rows)
    total = jnp.sum(xt, axis=1, keepdims=True)
    return jnp.broadcast_to(total, (width // group, group, rows)).reshape(width, rows).T


def row_group_sum(x, group):
    rows, width = x.shape
    xr = x.reshape(rows // group, group, width)
    total = jnp.sum(xr, axis=1, keepdims=True)
    return jnp.broadcast_to(total, (rows // group, group, width)).reshape(rows, width)


def place_kernel(group, recv, edge_at_ref, m_ref, g_ref):
    block = pl.program_id(0)
    firsts = g_ref.shape[0] // group

    def place(first, carry):
        row = pl.multiple_of(first * group, group)
        base = (block * firsts + first) * recv
        for second in range(recv):
            g_ref[pl.ds(row, group), second * group : (second + 1) * group] = m_ref[
                edge_at_ref[base + second]
            ]
        return carry

    lax.fori_loop(0, firsts, place, 0)


def place_grads(edge_at, blocks, total_rows, width, group):
    recv = width // group
    block = 128 if total_rows % 128 == 0 else total_rows
    return pl.pallas_call(
        functools.partial(place_kernel, group, recv),
        out_shape=jax.ShapeDtypeStruct((total_rows, width), blocks.dtype),
        grid_spec=pltpu.PrefetchScalarGridSpec(
            num_scalar_prefetch=1,
            grid=(total_rows // block,),
            in_specs=[pl.BlockSpec(blocks.shape, lambda b, e: (0, 0, 0))],
            out_specs=pl.BlockSpec((block, width), lambda b, e: (b, 0)),
        ),
        compiler_params=pltpu.CompilerParams(vmem_limit_bytes=32 * 1024 * 1024),
        cost_estimate=pl.CostEstimate(
            flops=0, transcendentals=0, bytes_accessed=2 * total_rows * width + 2 * blocks.size
        ),
    )(edge_at, blocks)


def softmax_bwd_kernel(group, score_scale, s_ref, g_ref, d_ref, dt_ref):
    expo = jnp.exp(s_ref[...])
    rows = expo / lane_group_sum(expo, group)
    cols = expo / row_group_sum(expo, group)
    grads = g_ref[...].astype(jnp.float32)
    d_rows = grads * cols
    d_cols = grads * rows
    d_scores = rows * (d_rows - lane_group_sum(d_rows * rows, group)) + cols * (
        d_cols - row_group_sum(d_cols * cols, group)
    )
    d_scaled = d_scores * score_scale
    d_ref[...] = d_scaled.astype(jnp.bfloat16)
    dt_ref[...] = d_scaled.T.astype(jnp.bfloat16)


def softmax_bwd(scores, grads, group, score_scale):
    total_rows, width = scores.shape
    block = 128 if total_rows % 128 == 0 else total_rows
    return pl.pallas_call(
        functools.partial(softmax_bwd_kernel, group, score_scale),
        out_shape=(
            jax.ShapeDtypeStruct((total_rows, width), jnp.bfloat16),
            jax.ShapeDtypeStruct((width, total_rows), jnp.bfloat16),
        ),
        grid=(total_rows // block,),
        in_specs=[
            pl.BlockSpec((block, width), lambda b: (b, 0)),
            pl.BlockSpec((block, width), lambda b: (b, 0)),
        ],
        out_specs=(
            pl.BlockSpec((block, width), lambda b: (b, 0)),
            pl.BlockSpec((width, block), lambda b: (0, b)),
        ),
        compiler_params=pltpu.CompilerParams(vmem_limit_bytes=48 * 1024 * 1024),
        cost_estimate=pl.CostEstimate(
            flops=30 * total_rows * width,
            transcendentals=total_rows * width,
            bytes_accessed=8 * total_rows * width,
        ),
    )(scores, grads)


def local(n_grp, n_sub, tokens, proj_weight, match_grad, edge_first, pair_second_image, send_pick):
    img_count, length, feat_width = tokens.shape
    recv = send_pick.shape[0]
    slots = recv // n_grp
    group_img = img_count * n_sub
    edge_count = edge_first.shape[0]
    grp_at = lax.axis_index("grp")
    sub_at = lax.axis_index("sub")

    normed, inv_rms, normed_b = normalize(tokens, proj_weight)

    if SUB_MODE == "perm":
        pool = jnp.concatenate(
            [normed_b]
            + [
                normalize(lax.ppermute(tokens, "sub", shift(n_sub, k)), proj_weight)[2]
                for k in range(1, n_sub)
            ],
            axis=0,
        )
        first_at = ((sub_at - edge_first // img_count) % n_sub) * img_count + edge_first % img_count
    elif SUB_MODE == "gather":
        pool = lax.all_gather(normed_b, "sub", axis=0, tiled=True)
        first_at = edge_first
    else:
        pool = lax.all_to_all(
            jnp.concatenate([normed_b] * n_sub, axis=0), "sub", split_axis=0, concat_axis=0, tiled=True
        )
        first_at = edge_first

    picks = send_pick.reshape(n_grp, slots)
    if GRP_MODE == "perm":
        order = picks[(grp_at + jnp.arange(n_grp, dtype=jnp.int32)) % n_grp].reshape(recv)
    else:
        order = send_pick
    outgoing = jnp.broadcast_to(tokens[img_count - 1], (recv, length, feat_width))
    for image in range(img_count - 2, -1, -1):
        outgoing = jnp.where(order[:, None, None] == image, tokens[image], outgoing)
    if GRP_MODE == "perm":
        received = jnp.concatenate(
            [outgoing[:slots]]
            + [
                lax.ppermute(outgoing[k * slots : (k + 1) * slots], "grp", shift(n_grp, k))
                for k in range(1, n_grp)
            ],
            axis=0,
        )
        second_at = ((grp_at - pair_second_image // slots) % n_grp) * slots + pair_second_image % slots
    else:
        received = normalize(
            lax.all_to_all(outgoing, "grp", split_axis=0, concat_axis=0, tiled=True), proj_weight
        )[2]
        second_at = pair_second_image

    pair_at = first_at * recv + second_at
    edge_ids = jnp.arange(edge_count, dtype=jnp.int32)
    edge_at = jnp.min(
        jnp.where(
            lax.broadcasted_iota(jnp.int32, (group_img * recv, edge_count), 0) == pair_at[None, :],
            edge_ids[None, :],
            edge_count,
        ),
        axis=1,
    )
    blocks = jnp.concatenate(
        [match_grad.reshape(edge_count, length, length), jnp.zeros((1, length, length), match_grad.dtype)],
        axis=0,
    )
    grads = place_grads(edge_at, blocks, group_img * length, recv * length, length)
    pool2 = pool.reshape(group_img * length, feat_width)
    recv2 = received.reshape(recv * length, feat_width)
    score_scale = 1.0 / (feat_width * SOFTMAX_COOLING)
    scores = (
        lax.dot_general(pool2, recv2, (((1,), (1,)), ((), ())), preferred_element_type=jnp.float32)
        * score_scale
    )
    d_scaled, d_scaled_t = softmax_bwd(scores, grads, length, score_scale)
    pool_total = jnp.dot(d_scaled, recv2, preferred_element_type=jnp.float32).reshape(
        group_img, length, feat_width
    )
    slot_total = jnp.dot(d_scaled_t, pool2, preferred_element_type=jnp.float32).reshape(
        recv, length, feat_width
    )
    pool_b = pool_total.astype(jnp.bfloat16)
    slot_b = slot_total.astype(jnp.bfloat16)

    if SUB_MODE == "perm":
        owned = pool_b[:img_count].astype(jnp.float32)
        for k in range(1, n_sub):
            owned = owned + lax.ppermute(
                pool_b[k * img_count : (k + 1) * img_count], "sub", shift(n_sub, -k)
            ).astype(jnp.float32)
    elif SUB_MODE == "a2a":
        back = lax.all_to_all(pool_b, "sub", split_axis=0, concat_axis=0, tiled=True).astype(jnp.float32)
        owned = jnp.sum(back.reshape(n_sub, img_count, length, feat_width), axis=0)
    else:
        owned = lax.psum_scatter(pool_b, "sub", scatter_dimension=0, tiled=True).astype(jnp.float32)

    if GRP_MODE == "perm":
        returned = jnp.concatenate(
            [slot_b[:slots]]
            + [
                lax.ppermute(slot_b[k * slots : (k + 1) * slots], "grp", shift(n_grp, -k))
                for k in range(1, n_grp)
            ],
            axis=0,
        )
    else:
        returned = lax.all_to_all(slot_b, "grp", split_axis=0, concat_axis=0, tiled=True)
    slot_images = order[:, None, None, None] == jnp.arange(img_count, dtype=jnp.int32)[None, :, None, None]
    incoming_gradient = owned + jnp.sum(
        jnp.where(slot_images, returned.astype(jnp.float32)[:, None], 0.0), axis=0
    )
    incoming_gradient = incoming_gradient.reshape(img_count * length, feat_width)
    feature_grad = (
        inv_rms
        * (
            incoming_gradient
            - normed * jnp.mean(incoming_gradient * normed, axis=-1, keepdims=True)
        )
    ).astype(jnp.bfloat16)
    token_grad = jnp.einsum(
        "nk,dk->nd", feature_grad, proj_weight, preferred_element_type=jnp.float32
    )
    return token_grad.astype(jnp.bfloat16).reshape(img_count, length, feat_width)


def solution(mesh):
    placed = (
        P(("grp", "sub"), None, None),
        P(),
        P(("grp", "sub"), None),
        P(("grp", "sub")),
        P(("grp", "sub")),
        P(("grp", "sub")),
    )
    n_grp = mesh.shape["grp"]
    n_sub = mesh.shape["sub"]

    def run(*args):
        return local(n_grp, n_sub, *args)

    return jax.shard_map(
        run, mesh=mesh, in_specs=placed, out_specs=P(("grp", "sub"), None, None), check_vma=False
    )
```

```python
import functools

import jax
import jax.numpy as jnp
from jax import lax
from jax.experimental import pallas as pl
from jax.experimental.pallas import tpu as pltpu
from jax.sharding import PartitionSpec as P

EPSILON = 1e-05
SOFTMAX_COOLING = 0.1
SUB_MODE = "perm"
GRP_MODE = "a2a"


def normalize(tokens, proj_weight):
    image_count, length, feat_width = tokens.shape
    feature = jnp.dot(
        tokens.reshape(image_count * length, feat_width),
        proj_weight,
        preferred_element_type=jnp.float32,
    )
    inv_rms = lax.rsqrt(jnp.mean(feature * feature, axis=-1, keepdims=True) + EPSILON)
    normed = feature * inv_rms
    return (normed, inv_rms, normed.astype(jnp.bfloat16).reshape(image_count, length, feat_width))


def shift(count, step):
    return [(i, (i + step) % count) for i in range(count)]


def partner(count, step):
    return [(i, i ^ step) for i in range(count)]


def lane_group_sum(x, group):
    rows, width = x.shape
    xt = x.T.reshape(width // group, group, rows)
    total = jnp.sum(xt, axis=1, keepdims=True)
    return jnp.broadcast_to(total, (width // group, group, rows)).reshape(width, rows).T


def row_group_sum(x, group):
    rows, width = x.shape
    xr = x.reshape(rows // group, group, width)
    total = jnp.sum(xr, axis=1, keepdims=True)
    return jnp.broadcast_to(total, (rows // group, group, width)).reshape(rows, width)


def place_kernel(group, recv, edge_at_ref, m_ref, g_ref):
    block = pl.program_id(0)
    firsts = g_ref.shape[0] // group

    def place(first, carry):
        row = pl.multiple_of(first * group, group)
        base = (block * firsts + first) * recv
        for second in range(recv):
            g_ref[pl.ds(row, group), second * group : (second + 1) * group] = m_ref[
                edge_at_ref[base + second]
            ]
        return carry

    lax.fori_loop(0, firsts, place, 0)


def place_grads(edge_at, blocks, total_rows, width, group):
    recv = width // group
    block = 128 if total_rows % 128 == 0 else total_rows
    return pl.pallas_call(
        functools.partial(place_kernel, group, recv),
        out_shape=jax.ShapeDtypeStruct((total_rows, width), blocks.dtype),
        grid_spec=pltpu.PrefetchScalarGridSpec(
            num_scalar_prefetch=1,
            grid=(total_rows // block,),
            in_specs=[pl.BlockSpec(blocks.shape, lambda b, e: (0, 0, 0))],
            out_specs=pl.BlockSpec((block, width), lambda b, e: (b, 0)),
        ),
        compiler_params=pltpu.CompilerParams(vmem_limit_bytes=32 * 1024 * 1024),
        cost_estimate=pl.CostEstimate(
            flops=0, transcendentals=0, bytes_accessed=2 * total_rows * width + 2 * blocks.size
        ),
    )(edge_at, blocks)


def softmax_bwd_kernel(group, score_scale, s_ref, g_ref, d_ref, dt_ref):
    expo = jnp.exp(s_ref[...])
    rows = expo / lane_group_sum(expo, group)
    cols = expo / row_group_sum(expo, group)
    grads = g_ref[...].astype(jnp.float32)
    d_rows = grads * cols
    d_cols = grads * rows
    d_scores = rows * (d_rows - lane_group_sum(d_rows * rows, group)) + cols * (
        d_cols - row_group_sum(d_cols * cols, group)
    )
    d_scaled = d_scores * score_scale
    d_ref[...] = d_scaled.astype(jnp.bfloat16)
    dt_ref[...] = d_scaled.T.astype(jnp.bfloat16)


def softmax_bwd(scores, grads, group, score_scale):
    total_rows, width = scores.shape
    block = 128 if total_rows % 128 == 0 else total_rows
    return pl.pallas_call(
        functools.partial(softmax_bwd_kernel, group, score_scale),
        out_shape=(
            jax.ShapeDtypeStruct((total_rows, width), jnp.bfloat16),
            jax.ShapeDtypeStruct((width, total_rows), jnp.bfloat16),
        ),
        grid=(total_rows // block,),
        in_specs=[
            pl.BlockSpec((block, width), lambda b: (b, 0)),
            pl.BlockSpec((block, width), lambda b: (b, 0)),
        ],
        out_specs=(
            pl.BlockSpec((block, width), lambda b: (b, 0)),
            pl.BlockSpec((width, block), lambda b: (0, b)),
        ),
        compiler_params=pltpu.CompilerParams(vmem_limit_bytes=48 * 1024 * 1024),
        cost_estimate=pl.CostEstimate(
            flops=30 * total_rows * width,
            transcendentals=total_rows * width,
            bytes_accessed=8 * total_rows * width,
        ),
    )(scores, grads)


def local(n_grp, n_sub, tokens, proj_weight, match_grad, edge_first, pair_second_image, send_pick):
    img_count, length, feat_width = tokens.shape
    recv = send_pick.shape[0]
    slots = recv // n_grp
    group_img = img_count * n_sub
    edge_count = edge_first.shape[0]
    grp_at = lax.axis_index("grp")
    sub_at = lax.axis_index("sub")

    normed, inv_rms, normed_b = normalize(tokens, proj_weight)

    paired = n_sub & (n_sub - 1) == 0

    def sub_to(k):
        return partner(n_sub, k) if paired else shift(n_sub, k)

    def sub_back(k):
        return partner(n_sub, k) if paired else shift(n_sub, -k)

    if SUB_MODE == "perm":
        pool = jnp.concatenate(
            [normed_b]
            + [
                normalize(lax.ppermute(tokens, "sub", sub_to(k)), proj_weight)[2]
                for k in range(1, n_sub)
            ],
            axis=0,
        )
        if paired:
            first_at = ((edge_first // img_count) ^ sub_at) * img_count + edge_first % img_count
        else:
            first_at = ((sub_at - edge_first // img_count) % n_sub) * img_count + edge_first % img_count
    elif SUB_MODE == "gather":
        pool = lax.all_gather(normed_b, "sub", axis=0, tiled=True)
        first_at = edge_first
    else:
        pool = lax.all_to_all(
            jnp.concatenate([normed_b] * n_sub, axis=0), "sub", split_axis=0, concat_axis=0, tiled=True
        )
        first_at = edge_first

    picks = send_pick.reshape(n_grp, slots)
    if GRP_MODE == "perm":
        order = picks[(grp_at + jnp.arange(n_grp, dtype=jnp.int32)) % n_grp].reshape(recv)
    else:
        order = send_pick
    outgoing = jnp.broadcast_to(tokens[img_count - 1], (recv, length, feat_width))
    for image in range(img_count - 2, -1, -1):
        outgoing = jnp.where(order[:, None, None] == image, tokens[image], outgoing)
    if GRP_MODE == "perm":
        received = jnp.concatenate(
            [outgoing[:slots]]
            + [
                lax.ppermute(outgoing[k * slots : (k + 1) * slots], "grp", shift(n_grp, k))
                for k in range(1, n_grp)
            ],
            axis=0,
        )
        second_at = ((grp_at - pair_second_image // slots) % n_grp) * slots + pair_second_image % slots
    else:
        received = normalize(
            lax.all_to_all(outgoing, "grp", split_axis=0, concat_axis=0, tiled=True), proj_weight
        )[2]
        second_at = pair_second_image

    pair_at = first_at * recv + second_at
    edge_ids = jnp.arange(edge_count, dtype=jnp.int32)
    edge_at = jnp.min(
        jnp.where(
            lax.broadcasted_iota(jnp.int32, (group_img * recv, edge_count), 0) == pair_at[None, :],
            edge_ids[None, :],
            edge_count,
        ),
        axis=1,
    )
    blocks = jnp.concatenate(
        [match_grad.reshape(edge_count, length, length), jnp.zeros((1, length, length), match_grad.dtype)],
        axis=0,
    )
    grads = place_grads(edge_at, blocks, group_img * length, recv * length, length)
    pool2 = pool.reshape(group_img * length, feat_width)
    recv2 = received.reshape(recv * length, feat_width)
    score_scale = 1.0 / (feat_width * SOFTMAX_COOLING)
    scores = (
        lax.dot_general(pool2, recv2, (((1,), (1,)), ((), ())), preferred_element_type=jnp.float32)
        * score_scale
    )
    d_scaled, d_scaled_t = softmax_bwd(scores, grads, length, score_scale)
    pool_total = jnp.dot(d_scaled, recv2, preferred_element_type=jnp.float32).reshape(
        group_img, length, feat_width
    )
    slot_total = jnp.dot(d_scaled_t, pool2, preferred_element_type=jnp.float32).reshape(
        recv, length, feat_width
    )
    pool_b = pool_total.astype(jnp.bfloat16)
    slot_b = slot_total.astype(jnp.bfloat16)

    if SUB_MODE == "perm":
        owned = pool_b[:img_count].astype(jnp.float32)
        for k in range(1, n_sub):
            owned = owned + lax.ppermute(
                pool_b[k * img_count : (k + 1) * img_count], "sub", sub_back(k)
            ).astype(jnp.float32)
    elif SUB_MODE == "a2a":
        back = lax.all_to_all(pool_b, "sub", split_axis=0, concat_axis=0, tiled=True).astype(jnp.float32)
        owned = jnp.sum(back.reshape(n_sub, img_count, length, feat_width), axis=0)
    else:
        owned = lax.psum_scatter(pool_b, "sub", scatter_dimension=0, tiled=True).astype(jnp.float32)

    if GRP_MODE == "perm":
        returned = jnp.concatenate(
            [slot_b[:slots]]
            + [
                lax.ppermute(slot_b[k * slots : (k + 1) * slots], "grp", shift(n_grp, -k))
                for k in range(1, n_grp)
            ],
            axis=0,
        )
    else:
        returned = lax.all_to_all(slot_b, "grp", split_axis=0, concat_axis=0, tiled=True)
    slot_images = order[:, None, None, None] == jnp.arange(img_count, dtype=jnp.int32)[None, :, None, None]
    incoming_gradient = owned + jnp.sum(
        jnp.where(slot_images, returned.astype(jnp.float32)[:, None], 0.0), axis=0
    )
    incoming_gradient = incoming_gradient.reshape(img_count * length, feat_width)
    feature_grad = (
        inv_rms
        * (
            incoming_gradient
            - normed * jnp.mean(incoming_gradient * normed, axis=-1, keepdims=True)
        )
    ).astype(jnp.bfloat16)
    token_grad = jnp.einsum(
        "nk,dk->nd", feature_grad, proj_weight, preferred_element_type=jnp.float32
    )
    return token_grad.astype(jnp.bfloat16).reshape(img_count, length, feat_width)


def solution(mesh):
    placed = (
        P(("grp", "sub"), None, None),
        P(),
        P(("grp", "sub"), None),
        P(("grp", "sub")),
        P(("grp", "sub")),
        P(("grp", "sub")),
    )
    n_grp = mesh.shape["grp"]
    n_sub = mesh.shape["sub"]

    def run(*args):
        return local(n_grp, n_sub, *args)

    return jax.shard_map(
        run, mesh=mesh, in_specs=placed, out_specs=P(("grp", "sub"), None, None), check_vma=False
    )
```

```python
import functools

import jax
import jax.numpy as jnp
from jax import lax
from jax.experimental import pallas as pl
from jax.experimental.pallas import tpu as pltpu
from jax.sharding import PartitionSpec as P

EPSILON = 1e-05
SOFTMAX_COOLING = 0.1
SUB_MODE = "perm"
GRP_MODE = "a2a"


def normalize(tokens, proj_weight):
    image_count, length, feat_width = tokens.shape
    feature = jnp.dot(
        tokens.reshape(image_count * length, feat_width),
        proj_weight,
        preferred_element_type=jnp.float32,
    )
    inv_rms = lax.rsqrt(jnp.mean(feature * feature, axis=-1, keepdims=True) + EPSILON)
    normed = feature * inv_rms
    return (normed, inv_rms, normed.astype(jnp.bfloat16).reshape(image_count, length, feat_width))


def shift(count, step):
    return [(i, (i + step) % count) for i in range(count)]


def partner(count, step):
    return [(i, i ^ step) for i in range(count)]


def lane_group_sum(x, group):
    rows, width = x.shape
    xt = x.T.reshape(width // group, group, rows)
    total = jnp.sum(xt, axis=1, keepdims=True)
    return jnp.broadcast_to(total, (width // group, group, rows)).reshape(width, rows).T


def row_group_sum(x, group):
    rows, width = x.shape
    xr = x.reshape(rows // group, group, width)
    total = jnp.sum(xr, axis=1, keepdims=True)
    return jnp.broadcast_to(total, (rows // group, group, width)).reshape(rows, width)


def place_kernel(group, recv, edge_at_ref, m_ref, g_ref):
    block = pl.program_id(0)
    firsts = g_ref.shape[0] // group

    def place(first, carry):
        row = pl.multiple_of(first * group, group)
        base = (block * firsts + first) * recv
        for second in range(recv):
            g_ref[pl.ds(row, group), second * group : (second + 1) * group] = m_ref[
                edge_at_ref[base + second]
            ]
        return carry

    lax.fori_loop(0, firsts, place, 0)


def place_grads(edge_at, blocks, total_rows, width, group):
    recv = width // group
    block = 128 if total_rows % 128 == 0 else total_rows
    return pl.pallas_call(
        functools.partial(place_kernel, group, recv),
        out_shape=jax.ShapeDtypeStruct((total_rows, width), blocks.dtype),
        grid_spec=pltpu.PrefetchScalarGridSpec(
            num_scalar_prefetch=1,
            grid=(total_rows // block,),
            in_specs=[pl.BlockSpec(blocks.shape, lambda b, e: (0, 0, 0))],
            out_specs=pl.BlockSpec((block, width), lambda b, e: (b, 0)),
        ),
        compiler_params=pltpu.CompilerParams(vmem_limit_bytes=32 * 1024 * 1024),
        cost_estimate=pl.CostEstimate(
            flops=0, transcendentals=0, bytes_accessed=2 * total_rows * width + 2 * blocks.size
        ),
    )(edge_at, blocks)


def softmax_bwd_kernel(group, score_scale, s_ref, g_ref, d_ref, dt_ref):
    expo = jnp.exp(s_ref[...])
    rows = expo / lane_group_sum(expo, group)
    cols = expo / row_group_sum(expo, group)
    grads = g_ref[...].astype(jnp.float32)
    d_rows = grads * cols
    d_cols = grads * rows
    d_scores = rows * (d_rows - lane_group_sum(d_rows * rows, group)) + cols * (
        d_cols - row_group_sum(d_cols * cols, group)
    )
    d_scaled = d_scores * score_scale
    d_ref[...] = d_scaled.astype(jnp.bfloat16)
    dt_ref[...] = d_scaled.T.astype(jnp.bfloat16)


def softmax_bwd(scores, grads, group, score_scale):
    total_rows, width = scores.shape
    block = 128 if total_rows % 128 == 0 else total_rows
    return pl.pallas_call(
        functools.partial(softmax_bwd_kernel, group, score_scale),
        out_shape=(
            jax.ShapeDtypeStruct((total_rows, width), jnp.bfloat16),
            jax.ShapeDtypeStruct((width, total_rows), jnp.bfloat16),
        ),
        grid=(total_rows // block,),
        in_specs=[
            pl.BlockSpec((block, width), lambda b: (b, 0)),
            pl.BlockSpec((block, width), lambda b: (b, 0)),
        ],
        out_specs=(
            pl.BlockSpec((block, width), lambda b: (b, 0)),
            pl.BlockSpec((width, block), lambda b: (0, b)),
        ),
        compiler_params=pltpu.CompilerParams(vmem_limit_bytes=48 * 1024 * 1024),
        cost_estimate=pl.CostEstimate(
            flops=30 * total_rows * width,
            transcendentals=total_rows * width,
            bytes_accessed=8 * total_rows * width,
        ),
    )(scores, grads)


def local(n_grp, n_sub, tokens, proj_weight, match_grad, edge_first, pair_second_image, send_pick):
    img_count, length, feat_width = tokens.shape
    recv = send_pick.shape[0]
    slots = recv // n_grp
    group_img = img_count * n_sub
    edge_count = edge_first.shape[0]
    grp_at = lax.axis_index("grp")
    sub_at = lax.axis_index("sub")

    normed, inv_rms, normed_b = normalize(tokens, proj_weight)

    paired = n_sub & (n_sub - 1) == 0

    def sub_to(k):
        return partner(n_sub, k) if paired else shift(n_sub, k)

    def sub_back(k):
        return partner(n_sub, k) if paired else shift(n_sub, -k)

    if SUB_MODE == "perm":
        pool = jnp.concatenate(
            [normed_b]
            + [
                normalize(lax.ppermute(tokens, "sub", sub_to(k)), proj_weight)[2]
                for k in range(1, n_sub)
            ],
            axis=0,
        )
        if paired:
            first_at = ((edge_first // img_count) ^ sub_at) * img_count + edge_first % img_count
        else:
            first_at = ((sub_at - edge_first // img_count) % n_sub) * img_count + edge_first % img_count
    elif SUB_MODE == "gather":
        pool = lax.all_gather(normed_b, "sub", axis=0, tiled=True)
        first_at = edge_first
    else:
        pool = lax.all_to_all(
            jnp.concatenate([normed_b] * n_sub, axis=0), "sub", split_axis=0, concat_axis=0, tiled=True
        )
        first_at = edge_first

    picks = send_pick.reshape(n_grp, slots)
    if GRP_MODE == "perm":
        order = picks[(grp_at + jnp.arange(n_grp, dtype=jnp.int32)) % n_grp].reshape(recv)
    else:
        order = send_pick
    chosen = order[:, None, None, None] == jnp.arange(img_count, dtype=jnp.int32)[None, :, None, None]
    outgoing = jnp.sum(
        jnp.where(chosen, tokens[None], jnp.zeros((), tokens.dtype)), axis=1
    ).astype(tokens.dtype)
    if GRP_MODE == "perm":
        received = jnp.concatenate(
            [outgoing[:slots]]
            + [
                lax.ppermute(outgoing[k * slots : (k + 1) * slots], "grp", shift(n_grp, k))
                for k in range(1, n_grp)
            ],
            axis=0,
        )
        second_at = ((grp_at - pair_second_image // slots) % n_grp) * slots + pair_second_image % slots
    else:
        received = normalize(
            lax.all_to_all(outgoing, "grp", split_axis=0, concat_axis=0, tiled=True), proj_weight
        )[2]
        second_at = pair_second_image

    pair_at = first_at * recv + second_at
    edge_ids = jnp.arange(edge_count, dtype=jnp.int32)
    edge_at = jnp.min(
        jnp.where(
            lax.broadcasted_iota(jnp.int32, (group_img * recv, edge_count), 0) == pair_at[None, :],
            edge_ids[None, :],
            edge_count,
        ),
        axis=1,
    )
    blocks = jnp.concatenate(
        [match_grad.reshape(edge_count, length, length), jnp.zeros((1, length, length), match_grad.dtype)],
        axis=0,
    )
    grads = place_grads(edge_at, blocks, group_img * length, recv * length, length)
    pool2 = pool.reshape(group_img * length, feat_width)
    recv2 = received.reshape(recv * length, feat_width)
    score_scale = 1.0 / (feat_width * SOFTMAX_COOLING)
    scores = (
        lax.dot_general(pool2, recv2, (((1,), (1,)), ((), ())), preferred_element_type=jnp.float32)
        * score_scale
    )
    d_scaled, d_scaled_t = softmax_bwd(scores, grads, length, score_scale)
    pool_total = jnp.dot(d_scaled, recv2, preferred_element_type=jnp.float32).reshape(
        group_img, length, feat_width
    )
    slot_total = jnp.dot(d_scaled_t, pool2, preferred_element_type=jnp.float32).reshape(
        recv, length, feat_width
    )
    pool_b = pool_total.astype(jnp.bfloat16)
    slot_b = slot_total.astype(jnp.bfloat16)

    if SUB_MODE == "perm":
        owned = pool_b[:img_count].astype(jnp.float32)
        for k in range(1, n_sub):
            owned = owned + lax.ppermute(
                pool_b[k * img_count : (k + 1) * img_count], "sub", sub_back(k)
            ).astype(jnp.float32)
    elif SUB_MODE == "a2a":
        back = lax.all_to_all(pool_b, "sub", split_axis=0, concat_axis=0, tiled=True).astype(jnp.float32)
        owned = jnp.sum(back.reshape(n_sub, img_count, length, feat_width), axis=0)
    else:
        owned = lax.psum_scatter(pool_b, "sub", scatter_dimension=0, tiled=True).astype(jnp.float32)

    if GRP_MODE == "perm":
        returned = jnp.concatenate(
            [slot_b[:slots]]
            + [
                lax.ppermute(slot_b[k * slots : (k + 1) * slots], "grp", shift(n_grp, -k))
                for k in range(1, n_grp)
            ],
            axis=0,
        )
    else:
        returned = lax.all_to_all(slot_b, "grp", split_axis=0, concat_axis=0, tiled=True)
    slot_images = order[:, None, None, None] == jnp.arange(img_count, dtype=jnp.int32)[None, :, None, None]
    incoming_gradient = owned + jnp.sum(
        jnp.where(slot_images, returned.astype(jnp.float32)[:, None], 0.0), axis=0
    )
    incoming_gradient = incoming_gradient.reshape(img_count * length, feat_width)
    feature_grad = (
        inv_rms
        * (
            incoming_gradient
            - normed * jnp.mean(incoming_gradient * normed, axis=-1, keepdims=True)
        )
    ).astype(jnp.bfloat16)
    token_grad = jnp.einsum(
        "nk,dk->nd", feature_grad, proj_weight, preferred_element_type=jnp.float32
    )
    return token_grad.astype(jnp.bfloat16).reshape(img_count, length, feat_width)


def solution(mesh):
    placed = (
        P(("grp", "sub"), None, None),
        P(),
        P(("grp", "sub"), None),
        P(("grp", "sub")),
        P(("grp", "sub")),
        P(("grp", "sub")),
    )
    n_grp = mesh.shape["grp"]
    n_sub = mesh.shape["sub"]

    def run(*args):
        return local(n_grp, n_sub, *args)

    return jax.shard_map(
        run, mesh=mesh, in_specs=placed, out_specs=P(("grp", "sub"), None, None), check_vma=False
    )
```
